32 devices in a mesh: grp: 2 (over y), aux: 16 (over z, x, core).
Axes of the slice: x: 2, y: 2, z: 4, core: 2. Of those that a mesh axis runs over, the one named last changes fastest.
Arguments:
- rhs: float32 [512, 2, 1024], P(('grp', 'aux')), parts along dimension 0, may hold values from -6 to 6
- occ_energy: float32 [512], P('grp'), parts along dimension 0, may hold values from -1.5 to -0.3
- vir_energy: float32 [2048], P('grp'), parts along dimension 0, may hold values from 0.2 to 3
- occ_ints: bfloat16 [128, 256, 256], P(('grp', 'aux')), parts along dimension 0, may hold values from -0.046875 to 0.046875
- vir_ints: bfloat16 [128, 1024, 1024], P(('grp', 'aux')), parts along dimension 0, may hold values from -0.1875 to 0.1875
Outputs:
- response: float32 [512, 2, 1024], P(('grp', 'aux')), parts along dimension 0
The draws below stay inside these ranges and needn't reach their ends.
There are 2 independent parts, one for each index of `grp`. The reference program is written for one: setup_inputs(seed, part) draws one part's arguments, and reference() takes and returns one part's arrays. A program takes and returns all parts, laid end to end along the dimension named above; each array names one. Nothing has to cross between parts.
All inputs are finite; a program needn't handle non-finite values.
Results may differ from the reference program's by a relative error of at most 0.0015.
Values may be sent and summed in bfloat16 or wider, within the bound.
No kernel may reach another device: no remote copies, remote signals or barrier semaphores. Data moves between devices by JAX's collectives and lax.ppermute only.
A program may use at most 64 MiB of HBM per device.

```python
import jax
import jax.numpy as jnp
from jax import lax

NOCC = 256
NVIR = 1024
NSTATE = 2
ITERS = 2
NAUX = 64


def strengthened(entries, own_key, source, target, shards_of, factor):
    def block_of(axis_at):
        return (jnp.arange(entries.shape[axis_at]) // (entries.shape[axis_at] // shards_of)).reshape((-1,) + (1,) * (entries.ndim - 1 - axis_at))

    one_side = jax.random.permutation(own_key, shards_of)[block_of(target)]
    far = (block_of(target) + shards_of // 2) % shards_of
    return jnp.where((block_of(source) == one_side) | (block_of(source) == far), factor * entries, entries)


def shard_levels(own_key, extent, shards, least, top_value):
    level = 1.0
    for axis_at, parts in shards:
        draws = jax.random.uniform(jax.random.fold_in(jax.random.fold_in(own_key, 6), axis_at), (parts,), jnp.float32, least / len(shards), top_value / len(shards))
        level = level * jnp.repeat(jnp.exp(draws), extent[axis_at] // parts).reshape((-1,) + (1,) * (len(extent) - 1 - axis_at))
    return level


def noise(key, extent, spread, most, split=(), dtype=jnp.bfloat16):
    gain = shard_levels(key, extent, split, -0.22, 0.18) if split else 1.0
    drawn = jax.random.normal(key, extent, jnp.float32) * spread * gain
    return jnp.minimum(jnp.maximum(drawn, -most), most).astype(dtype)


def gaussian_with(own_key, dims, scale, reach, split, heavy, dtype=jnp.bfloat16):
    result = scale * jax.random.normal(own_key, dims, jnp.float32)
    if split:
        result = result * shard_levels(own_key, dims, split, -0.22, 0.18)
    return jnp.clip(strengthened(result, jax.random.fold_in(own_key, 3), *heavy), -reach, reach).astype(dtype)


def setup_inputs(seed: int = 0, part: int = 0) -> dict:
    arg_keys = jax.random.split(jax.random.key(seed), 6)
    part_splits = jax.random.split(jax.random.fold_in(arg_keys[5], part), 6)
    rhs = noise(part_splits[0], (NOCC, NSTATE, NVIR), 1.0, 6.0, ((0, 16),), jnp.float32)
    occ_energy = jnp.clip(jax.random.uniform(part_splits[1], (NOCC,), jnp.float32, -1.5, -0.3), -1.5, -0.3)
    vir_energy = jnp.clip(jax.random.uniform(part_splits[2], (NVIR,), jnp.float32, 0.2, 3.0), 0.2, 3.0)
    occ_ints = gaussian_with(part_splits[3], (NAUX, NOCC, NOCC), (2 * NOCC * NAUX) ** -0.5, 0.046875, ((0, 16),), (0, 1, 16, 2.0))
    vir_ints = noise(part_splits[4], (NAUX, NVIR, NVIR), NVIR ** -0.5, 0.1875, ((0, 16),))
    return {"rhs": rhs, "occ_energy": occ_energy, "vir_energy": vir_energy, "occ_ints": occ_ints, "vir_ints": vir_ints}


def reference(rhs, occ_energy, vir_energy, occ_ints, vir_ints):
    denom = vir_energy[None, None, :] - occ_energy[:, None, None]
    response = rhs / denom
    for step in range(ITERS):
        rounded = response.astype(jnp.bfloat16).reshape(NOCC, NSTATE * NVIR)

        def accumulate(total, pair):
            occ_block, vir_block = pair
            half = jnp.dot(occ_block, rounded, preferred_element_type=jnp.float32).astype(jnp.bfloat16)
            half = half.reshape(NOCC * NSTATE, NVIR)
            term = lax.dot_general(half, vir_block, (((1,), (1,)), ((), ())), preferred_element_type=jnp.float32)
            return total + term, None

        start = jnp.zeros((NOCC * NSTATE, NVIR), jnp.float32)
        exchange, unused = lax.scan(accumulate, start, (occ_ints, vir_ints))
        exchange = exchange.reshape(NOCC, NSTATE, NVIR)
        response = 0.4 * response + 0.6 * (rhs - exchange) / denom
    return response
```

```python
import jax
import jax.numpy as jnp
from jax import lax
from jax.sharding import PartitionSpec as P

ITERS = 2


def gather_rows(x, n):
    me = lax.axis_index("aux")
    acc = x[None]
    k = n.bit_length() - 2
    while k >= 0:
        bit = (me >> k) & 1
        theirs = lax.ppermute(acc, "aux", [(d, d ^ (1 << k)) for d in range(n)])
        lo = jnp.where(bit == 0, acc, theirs)
        hi = jnp.where(bit == 0, theirs, acc)
        acc = jnp.stack([lo, hi], axis=1).reshape((-1,) + x.shape)
        k -= 1
    return acc.reshape((n * x.shape[0],) + x.shape[1:])


def scatter_sum(part, n):
    me = lax.axis_index("aux")
    rows = part.shape[0] // n
    acc = part.reshape((n, rows) + part.shape[1:])
    k = 0
    while (1 << k) < n:
        bit = (me >> k) & 1
        pairs = acc.reshape((acc.shape[0] // 2, 2) + acc.shape[1:])
        keep = lax.dynamic_index_in_dim(pairs, bit, axis=1, keepdims=False)
        send = lax.dynamic_index_in_dim(pairs, 1 - bit, axis=1, keepdims=False)
        acc = keep + lax.ppermute(send, "aux", [(d, d ^ (1 << k)) for d in range(n)])
        k += 1
    return acc[0]


def shards(rhs, occ_energy, vir_energy, occ_ints, vir_ints):
    own_rows = rhs.shape[0]
    states = rhs.shape[1]
    nvir = rhs.shape[2]
    local_aux = occ_ints.shape[0]
    nocc = occ_ints.shape[1]
    n = nocc // own_rows
    assert n & (n - 1) == 0
    position = lax.axis_index("aux")
    my_occ = lax.dynamic_slice_in_dim(occ_energy, position * own_rows, own_rows, 0)
    denom = vir_energy[None, None, :] - my_occ[:, None, None]
    response = rhs / denom
    for step in range(ITERS):
        rounded = response.astype(jnp.bfloat16)
        piece = gather_rows(rounded, n)
        flat = piece.reshape(nocc, states * nvir)
        half = jnp.einsum("pij,jk->pik", occ_ints, flat, preferred_element_type=jnp.float32)
        half = half.astype(jnp.bfloat16).reshape(local_aux, nocc, states, nvir)
        part = lax.dot_general(
            half, vir_ints, (((0, 3), (0, 2)), ((), ())), preferred_element_type=jnp.float32
        )
        exchange = scatter_sum(part, n)
        response = 0.4 * response + 0.6 * (rhs - exchange) / denom
    return response


def solution(mesh):
    in_specs = (
        P(("grp", "aux"), None, None),
        P("grp"),
        P("grp"),
        P(("grp", "aux"), None, None),
        P(("grp", "aux"), None, None),
    )
    out_specs = P(("grp", "aux"), None, None)
    return jax.shard_map(shards, mesh=mesh, in_specs=in_specs, out_specs=out_specs, check_vma=False)
```

```python
import functools

import jax
import jax.numpy as jnp
from jax import lax
from jax.experimental import pallas as pl
from jax.experimental.pallas import tpu as pltpu
from jax.sharding import PartitionSpec as P

ITERS = 2


def gather_rows(x, n):
    me = lax.axis_index("aux")
    acc = x[None]
    k = n.bit_length() - 2
    while k >= 0:
        bit = (me >> k) & 1
        theirs = lax.ppermute(acc, "aux", [(d, d ^ (1 << k)) for d in range(n)])
        lo = jnp.where(bit == 0, acc, theirs)
        hi = jnp.where(bit == 0, theirs, acc)
        acc = jnp.stack([lo, hi], axis=1).reshape((-1,) + x.shape)
        k -= 1
    return acc.reshape((n * x.shape[0],) + x.shape[1:])


def scatter_sum(part, n):
    me = lax.axis_index("aux")
    rows = part.shape[0] // n
    acc = part.reshape((n, rows) + part.shape[1:])
    k = 0
    while (1 << k) < n:
        bit = (me >> k) & 1
        pairs = acc.reshape((acc.shape[0] // 2, 2) + acc.shape[1:])
        keep = lax.dynamic_index_in_dim(pairs, bit, axis=1, keepdims=False)
        send = lax.dynamic_index_in_dim(pairs, 1 - bit, axis=1, keepdims=False)
        acc = keep + lax.ppermute(send, "aux", [(d, d ^ (1 << k)) for d in range(n)])
        k += 1
    return acc[0]


def exchange_kernel(states, occ_ref, r_ref, vir_ref, out_ref):
    @pl.when(pl.program_id(0) == 0)
    def _():
        out_ref[...] = jnp.zeros_like(out_ref)

    half = jnp.dot(occ_ref[0], r_ref[...], preferred_element_type=jnp.float32).astype(jnp.bfloat16)
    nvir = vir_ref.shape[1]
    vir = vir_ref[0]
    for s in range(states):
        cols = slice(s * nvir, (s + 1) * nvir)
        out_ref[:, cols] += lax.dot_general(
            half[:, cols], vir, (((1,), (1,)), ((), ())), preferred_element_type=jnp.float32
        )


def exchange_part(occ_ints, flat, vir_ints, states):
    local_aux, nocc, _ = occ_ints.shape
    nvir = vir_ints.shape[1]
    width = states * nvir
    return pl.pallas_call(
        functools.partial(exchange_kernel, states),
        grid=(local_aux,),
        in_specs=[
            pl.BlockSpec((1, nocc, nocc), lambda p: (p, 0, 0)),
            pl.BlockSpec((nocc, width), lambda p: (0, 0)),
            pl.BlockSpec((1, nvir, nvir), lambda p: (p, 0, 0)),
        ],
        out_specs=pl.BlockSpec((nocc, width), lambda p: (0, 0)),
        out_shape=jax.ShapeDtypeStruct((nocc, width), jnp.float32),
        compiler_params=pltpu.CompilerParams(dimension_semantics=("arbitrary",)),
    )(occ_ints, flat, vir_ints)


def shards(rhs, occ_energy, vir_energy, occ_ints, vir_ints):
    own_rows = rhs.shape[0]
    states = rhs.shape[1]
    nvir = rhs.shape[2]
    nocc = occ_ints.shape[1]
    n = nocc // own_rows
    assert n & (n - 1) == 0
    position = lax.axis_index("aux")
    my_occ = lax.dynamic_slice_in_dim(occ_energy, position * own_rows, own_rows, 0)
    denom = vir_energy[None, None, :] - my_occ[:, None, None]
    response = rhs / denom
    for step in range(ITERS):
        rounded = response.astype(jnp.bfloat16).reshape(own_rows, states * nvir)
        flat = gather_rows(rounded, n)
        part = exchange_part(occ_ints, flat, vir_ints, states)
        exchange = scatter_sum(part, n).reshape(own_rows, states, nvir)
        response = 0.4 * response + 0.6 * (rhs - exchange) / denom
    return response


def solution(mesh):
    in_specs = (
        P(("grp", "aux"), None, None),
        P("grp"),
        P("grp"),
        P(("grp", "aux"), None, None),
        P(("grp", "aux"), None, None),
    )
    out_specs = P(("grp", "aux"), None, None)
    return jax.shard_map(shards, mesh=mesh, in_specs=in_specs, out_specs=out_specs, check_vma=False)
```

```python
import functools

import jax
import jax.numpy as jnp
from jax import lax
from jax.experimental import pallas as pl
from jax.experimental.pallas import tpu as pltpu
from jax.sharding import PartitionSpec as P

ITERS = 2


def bit_orders(m, descending):
    order0 = list(range(1, m))
    order1 = list(order0)
    if len(order1) >= 2:
        order1[0], order1[1] = order1[1], order1[0]
    if descending:
        return order0[::-1] + [0], order1[::-1] + [0]
    return [0] + order0, [0] + order1


def partners(n, b0, b1):
    return [(d, d ^ (1 << (b1 if d & 1 else b0))) for d in range(n)]


def gather_rows(x, n):
    m = n.bit_length() - 1
    me = lax.axis_index("aux")
    odd = (me & 1) == 1
    order0, order1 = bit_orders(m, True)
    acc = x[None]
    have0, have1 = [], []
    for b0, b1 in zip(order0, order1):
        bit = jnp.where(odd, (me >> b1) & 1, (me >> b0) & 1)
        theirs = lax.ppermute(acc, "aux", partners(n, b0, b1))
        lo = jnp.where(bit == 0, acc, theirs)
        hi = jnp.where(bit == 0, theirs, acc)
        at0 = sum(1 for b in have0 if b > b0)
        at1 = sum(1 for b in have1 if b > b1)
        lead = len(have0)
        lo = lo.reshape((2,) * lead + x.shape) if lead else lo[0]
        hi = hi.reshape((2,) * lead + x.shape) if lead else hi[0]
        new0 = jnp.stack([lo, hi], axis=at0)
        if at1 == at0:
            acc = new0
        else:
            acc = jnp.where(odd, jnp.stack([lo, hi], axis=at1), new0)
        have0 = sorted(have0 + [b0], reverse=True)
        have1 = sorted(have1 + [b1], reverse=True)
        acc = acc.reshape((-1,) + x.shape)
    return acc.reshape((n * x.shape[0],) + x.shape[1:])


def scatter_sum(part, n):
    m = n.bit_length() - 1
    me = lax.axis_index("aux")
    odd = (me & 1) == 1
    rows = part.shape[0] // n
    order0, order1 = bit_orders(m, False)
    acc = part.reshape((2,) * m + (rows,) + part.shape[1:])
    axes0 = list(range(m - 1, -1, -1))
    axes1 = list(axes0)
    for b0, b1 in zip(order0, order1):
        at0, at1 = axes0.index(b0), axes1.index(b1)
        bit0, bit1 = (me >> b0) & 1, (me >> b1) & 1
        if at0 == at1:
            bit = jnp.where(odd, bit1, bit0)
            keep = lax.dynamic_index_in_dim(acc, bit, axis=at0, keepdims=False)
            send = lax.dynamic_index_in_dim(acc, 1 - bit, axis=at0, keepdims=False)
        else:
            keep = jnp.where(
                odd,
                lax.dynamic_index_in_dim(acc, bit1, axis=at1, keepdims=False),
                lax.dynamic_index_in_dim(acc, bit0, axis=at0, keepdims=False),
            )
            send = jnp.where(
                odd,
                lax.dynamic_index_in_dim(acc, 1 - bit1, axis=at1, keepdims=False),
                lax.dynamic_index_in_dim(acc, 1 - bit0, axis=at0, keepdims=False),
            )
        acc = keep + lax.ppermute(send, "aux", partners(n, b0, b1))
        axes0.pop(at0)
        axes1.pop(at1)
    return acc


def exchange_kernel(states, occ_ref, r_ref, vir_ref, out_ref):
    @pl.when(pl.program_id(0) == 0)
    def _():
        out_ref[...] = jnp.zeros_like(out_ref)

    half = jnp.dot(occ_ref[0], r_ref[...], preferred_element_type=jnp.float32).astype(jnp.bfloat16)
    nvir = vir_ref.shape[1]
    vir = vir_ref[0]
    for s in range(states):
        cols = slice(s * nvir, (s + 1) * nvir)
        out_ref[:, cols] += lax.dot_general(
            half[:, cols], vir, (((1,), (1,)), ((), ())), preferred_element_type=jnp.float32
        )


def exchange_part(occ_ints, flat, vir_ints, states):
    local_aux, nocc, _ = occ_ints.shape
    nvir = vir_ints.shape[1]
    width = states * nvir
    return pl.pallas_call(
        functools.partial(exchange_kernel, states),
        grid=(local_aux,),
        in_specs=[
            pl.BlockSpec((1, nocc, nocc), lambda p: (p, 0, 0)),
            pl.BlockSpec((nocc, width), lambda p: (0, 0)),
            pl.BlockSpec((1, nvir, nvir), lambda p: (p, 0, 0)),
        ],
        out_specs=pl.BlockSpec((nocc, width), lambda p: (0, 0)),
        out_shape=jax.ShapeDtypeStruct((nocc, width), jnp.float32),
        compiler_params=pltpu.CompilerParams(dimension_semantics=("arbitrary",)),
    )(occ_ints, flat, vir_ints)


def shards(rhs, occ_energy, vir_energy, occ_ints, vir_ints):
    own_rows = rhs.shape[0]
    states = rhs.shape[1]
    nvir = rhs.shape[2]
    nocc = occ_ints.shape[1]
    n = nocc // own_rows
    assert n & (n - 1) == 0
    position = lax.axis_index("aux")
    my_occ = lax.dynamic_slice_in_dim(occ_energy, position * own_rows, own_rows, 0)
    denom = vir_energy[None, None, :] - my_occ[:, None, None]
    response = rhs / denom
    for step in range(ITERS):
        rounded = response.astype(jnp.bfloat16).reshape(own_rows, states * nvir)
        flat = gather_rows(rounded, n)
        part = exchange_part(occ_ints, flat, vir_ints, states)
        exchange = scatter_sum(part, n).reshape(own_rows, states, nvir)
        response = 0.4 * response + 0.6 * (rhs - exchange) / denom
    return response


def solution(mesh):
    in_specs = (
        P(("grp", "aux"), None, None),
        P("grp"),
        P("grp"),
        P(("grp", "aux"), None, None),
        P(("grp", "aux"), None, None),
    )
    out_specs = P(("grp", "aux"), None, None)
    return jax.shard_map(shards, mesh=mesh, in_specs=in_specs, out_specs=out_specs, check_vma=False)
```

```python
import functools

import jax
import jax.numpy as jnp
from jax import lax
from jax.experimental import pallas as pl
from jax.experimental.pallas import tpu as pltpu
from jax.sharding import PartitionSpec as P

ITERS = 2


def bit_orders(m, descending):
    order0 = list(range(1, m))
    order1 = list(order0)
    if len(order1) >= 2:
        order1[0], order1[1] = order1[1], order1[0]
    if descending:
        return order0[::-1] + [0], order1[::-1] + [0]
    return [0] + order0, [0] + order1


def partners(n, b0, b1):
    return [(d, d ^ (1 << (b1 if d & 1 else b0))) for d in range(n)]


def gather_rows(x, n):
    m = n.bit_length() - 1
    me = lax.axis_index("aux")
    odd = (me & 1) == 1
    order0, order1 = bit_orders(m, True)
    acc = x[None]
    have0, have1 = [], []
    for b0, b1 in zip(order0, order1):
        bit = jnp.where(odd, (me >> b1) & 1, (me >> b0) & 1)
        theirs = lax.ppermute(acc, "aux", partners(n, b0, b1))
        lo = jnp.where(bit == 0, acc, theirs)
        hi = jnp.where(bit == 0, theirs, acc)
        at0 = sum(1 for b in have0 if b > b0)
        at1 = sum(1 for b in have1 if b > b1)
        lead = len(have0)
        lo = lo.reshape((2,) * lead + x.shape) if lead else lo[0]
        hi = hi.reshape((2,) * lead + x.shape) if lead else hi[0]
        new0 = jnp.stack([lo, hi], axis=at0)
        if at1 == at0:
            acc = new0
        else:
            acc = jnp.where(odd, jnp.stack([lo, hi], axis=at1), new0)
        have0 = sorted(have0 + [b0], reverse=True)
        have1 = sorted(have1 + [b1], reverse=True)
        acc = acc.reshape((-1,) + x.shape)
    return acc.reshape((n * x.shape[0],) + x.shape[1:])


def scatter_sum(part, n):
    m = n.bit_length() - 1
    me = lax.axis_index("aux")
    odd = (me & 1) == 1
    rows = part.shape[0] // n
    order0, order1 = bit_orders(m, False)
    acc = part.reshape((2,) * m + (rows,) + part.shape[1:])
    axes0 = list(range(m - 1, -1, -1))
    axes1 = list(axes0)
    for b0, b1 in zip(order0, order1):
        at0, at1 = axes0.index(b0), axes1.index(b1)
        bit0, bit1 = (me >> b0) & 1, (me >> b1) & 1
        if at0 == at1:
            bit = jnp.where(odd, bit1, bit0)
            keep = lax.dynamic_index_in_dim(acc, bit, axis=at0, keepdims=False)
            send = lax.dynamic_index_in_dim(acc, 1 - bit, axis=at0, keepdims=False)
        else:
            keep = jnp.where(
                odd,
                lax.dynamic_index_in_dim(acc, bit1, axis=at1, keepdims=False),
                lax.dynamic_index_in_dim(acc, bit0, axis=at0, keepdims=False),
            )
            send = jnp.where(
                odd,
                lax.dynamic_index_in_dim(acc, 1 - bit1, axis=at1, keepdims=False),
                lax.dynamic_index_in_dim(acc, 1 - bit0, axis=at0, keepdims=False),
            )
        acc = keep + lax.ppermute(send, "aux", partners(n, b0, b1))
        axes0.pop(at0)
        axes1.pop(at1)
    return acc


def exchange_kernel(states, occ_ref, r_ref, vir_ref, out_ref):
    @pl.when(pl.program_id(0) == 0)
    def _():
        out_ref[...] = jnp.zeros_like(out_ref)

    half = jnp.dot(occ_ref[0], r_ref[...], preferred_element_type=jnp.float32).astype(jnp.bfloat16)
    nvir = vir_ref.shape[1]
    vir = vir_ref[0]
    for s in range(states):
        cols = slice(s * nvir, (s + 1) * nvir)
        out_ref[:, cols] += lax.dot_general(
            half[:, cols], vir, (((1,), (1,)), ((), ())), preferred_element_type=jnp.float32
        )


def exchange_part(occ_ints, flat, vir_ints, states):
    local_aux, nocc, _ = occ_ints.shape
    nvir = vir_ints.shape[1]
    width = states * nvir
    return pl.pallas_call(
        functools.partial(exchange_kernel, states),
        grid=(local_aux,),
        in_specs=[
            pl.BlockSpec((1, nocc, nocc), lambda p: (p, 0, 0)),
            pl.BlockSpec((nocc, width), lambda p: (0, 0)),
            pl.BlockSpec((1, nvir, nvir), lambda p: (p, 0, 0)),
        ],
        out_specs=pl.BlockSpec((nocc, width), lambda p: (0, 0)),
        out_shape=jax.ShapeDtypeStruct((nocc, width), jnp.float32),
        compiler_params=pltpu.CompilerParams(dimension_semantics=("arbitrary",)),
    )(occ_ints, flat, vir_ints)


def shards(rhs, occ_energy, vir_energy, occ_ints, vir_ints):
    own_rows = rhs.shape[0]
    states = rhs.shape[1]
    nvir = rhs.shape[2]
    nocc = occ_ints.shape[1]
    n = nocc // own_rows
    assert n & (n - 1) == 0
    position = lax.axis_index("aux")
    my_occ = lax.dynamic_slice_in_dim(occ_energy, position * own_rows, own_rows, 0)
    denom = vir_energy[None, None, :] - my_occ[:, None, None]
    finals = []
    for state in range(states):
        own_rhs = rhs[:, state, :]
        own_denom = denom[:, 0, :]
        resp = own_rhs / own_denom
        for step in range(ITERS):
            rounded = resp.astype(jnp.bfloat16)
            flat = gather_rows(rounded, n)
            part = exchange_part(occ_ints, flat, vir_ints, 1)
            exchange = scatter_sum(part, n)
            resp = 0.4 * resp + 0.6 * (own_rhs - exchange) / own_denom
        finals.append(resp)
    response = jnp.stack(finals, axis=1)
    return response


def solution(mesh):
    in_specs = (
        P(("grp", "aux"), None, None),
        P("grp"),
        P("grp"),
        P(("grp", "aux"), None, None),
        P(("grp", "aux"), None, None),
    )
    out_specs = P(("grp", "aux"), None, None)
    return jax.shard_map(shards, mesh=mesh, in_specs=in_specs, out_specs=out_specs, check_vma=False)
```

```python
import functools

import jax
import jax.numpy as jnp
from jax import lax
from jax.experimental import pallas as pl
from jax.experimental.pallas import tpu as pltpu
from jax.sharding import PartitionSpec as P

ITERS = 2


def bit_orders(m, descending):
    order0 = list(range(1, m))
    order1 = list(order0)
    if len(order1) >= 2:
        order1[0], order1[1] = order1[1], order1[0]
    if descending:
        return order0[::-1] + [0], order1[::-1] + [0]
    return [0] + order0, [0] + order1


def partners(n, b0, b1):
    return [(d, d ^ (1 << (b1 if d & 1 else b0))) for d in range(n)]


def gather_rows(x, n):
    m = n.bit_length() - 1
    me = lax.axis_index("aux")
    odd = (me & 1) == 1
    order0, order1 = bit_orders(m, True)
    acc = x[None]
    have0, have1 = [], []
    for b0, b1 in zip(order0[:-1], order1[:-1]):
        bit = jnp.where(odd, (me >> b1) & 1, (me >> b0) & 1)
        theirs = lax.ppermute(acc, "aux", partners(n, b0, b1))
        lo = jnp.where(bit == 0, acc, theirs)
        hi = jnp.where(bit == 0, theirs, acc)
        at0 = sum(1 for b in have0 if b > b0)
        at1 = sum(1 for b in have1 if b > b1)
        lead = len(have0)
        lo = lo.reshape((2,) * lead + x.shape) if lead else lo[0]
        hi = hi.reshape((2,) * lead + x.shape) if lead else hi[0]
        new0 = jnp.stack([lo, hi], axis=at0)
        if at1 == at0:
            acc = new0
        else:
            acc = jnp.where(odd, jnp.stack([lo, hi], axis=at1), new0)
        have0 = sorted(have0 + [b0], reverse=True)
        have1 = sorted(have1 + [b1], reverse=True)
        acc = acc.reshape((-1,) + x.shape)
    theirs = lax.ppermute(acc, "aux", partners(n, 0, 0))
    return jnp.concatenate([acc, theirs], axis=0).reshape((n * x.shape[0],) + x.shape[1:])


def scatter_sum(part, n):
    m = n.bit_length() - 1
    me = lax.axis_index("aux")
    odd = (me & 1) == 1
    half = part.shape[0] // 2
    rows = part.shape[0] // n
    order0, order1 = bit_orders(m, False)
    shape = (2,) * (m - 1) + (rows,) + part.shape[1:]
    acc = part[:half].reshape(shape) + lax.ppermute(part[half:].reshape(shape), "aux", partners(n, 0, 0))
    axes0 = list(range(m - 1, 0, -1))
    axes1 = list(axes0)
    for b0, b1 in zip(order0[1:], order1[1:]):
        at0, at1 = axes0.index(b0), axes1.index(b1)
        bit0, bit1 = (me >> b0) & 1, (me >> b1) & 1
        if at0 == at1:
            bit = jnp.where(odd, bit1, bit0)
            keep = lax.dynamic_index_in_dim(acc, bit, axis=at0, keepdims=False)
            send = lax.dynamic_index_in_dim(acc, 1 - bit, axis=at0, keepdims=False)
        else:
            keep = jnp.where(
                odd,
                lax.dynamic_index_in_dim(acc, bit1, axis=at1, keepdims=False),
                lax.dynamic_index_in_dim(acc, bit0, axis=at0, keepdims=False),
            )
            send = jnp.where(
                odd,
                lax.dynamic_index_in_dim(acc, 1 - bit1, axis=at1, keepdims=False),
                lax.dynamic_index_in_dim(acc, 1 - bit0, axis=at0, keepdims=False),
            )
        acc = keep + lax.ppermute(send, "aux", partners(n, b0, b1))
        axes0.pop(at0)
        axes1.pop(at1)
    return acc


def order_occ_ints(occ_ints, n, core):
    local_aux, nocc, _ = occ_ints.shape
    rows = nocc // n
    o = occ_ints.reshape(local_aux, n // 2, 2, rows, nocc)
    even, odd = o[:, :, 0], o[:, :, 1]
    mine = core == 0
    o = jnp.stack([jnp.where(mine, even, odd), jnp.where(mine, odd, even)], axis=1)
    o = o.reshape(local_aux, nocc, n // 2, 2, rows)
    even, odd = o[:, :, :, 0], o[:, :, :, 1]
    o = jnp.stack([jnp.where(mine, even, odd), jnp.where(mine, odd, even)], axis=2)
    return o.reshape(local_aux, nocc, nocc)


def exchange_kernel(states, occ_ref, r_ref, vir_ref, out_ref):
    @pl.when(pl.program_id(0) == 0)
    def _():
        out_ref[...] = jnp.zeros_like(out_ref)

    half = jnp.dot(occ_ref[0], r_ref[...], preferred_element_type=jnp.float32).astype(jnp.bfloat16)
    nvir = vir_ref.shape[1]
    vir = vir_ref[0]
    for s in range(states):
        cols = slice(s * nvir, (s + 1) * nvir)
        out_ref[:, cols] += lax.dot_general(
            half[:, cols], vir, (((1,), (1,)), ((), ())), preferred_element_type=jnp.float32
        )


def exchange_part(occ_ints, flat, vir_ints, states):
    local_aux, nocc, _ = occ_ints.shape
    nvir = vir_ints.shape[1]
    width = states * nvir
    return pl.pallas_call(
        functools.partial(exchange_kernel, states),
        grid=(local_aux,),
        in_specs=[
            pl.BlockSpec((1, nocc, nocc), lambda p: (p, 0, 0)),
            pl.BlockSpec((nocc, width), lambda p: (0, 0)),
            pl.BlockSpec((1, nvir, nvir), lambda p: (p, 0, 0)),
        ],
        out_specs=pl.BlockSpec((nocc, width), lambda p: (0, 0)),
        out_shape=jax.ShapeDtypeStruct((nocc, width), jnp.float32),
        compiler_params=pltpu.CompilerParams(dimension_semantics=("arbitrary",)),
    )(occ_ints, flat, vir_ints)


def shards(rhs, occ_energy, vir_energy, occ_ints, vir_ints):
    own_rows = rhs.shape[0]
    states = rhs.shape[1]
    nvir = rhs.shape[2]
    nocc = occ_ints.shape[1]
    n = nocc // own_rows
    assert n & (n - 1) == 0
    position = lax.axis_index("aux")
    my_occ = lax.dynamic_slice_in_dim(occ_energy, position * own_rows, own_rows, 0)
    denom = vir_energy[None, None, :] - my_occ[:, None, None]
    ordered_occ = order_occ_ints(occ_ints, n, position & 1)
    finals = []
    for state in range(states):
        own_rhs = rhs[:, state, :]
        own_denom = denom[:, 0, :]
        resp = own_rhs / own_denom
        for step in range(ITERS):
            rounded = resp.astype(jnp.bfloat16)
            flat = gather_rows(rounded, n)
            part = exchange_part(ordered_occ, flat, vir_ints, 1)
            exchange = scatter_sum(part, n)
            resp = 0.4 * resp + 0.6 * (own_rhs - exchange) / own_denom
        finals.append(resp)
    response = jnp.stack(finals, axis=1)
    return response


def solution(mesh):
    in_specs = (
        P(("grp", "aux"), None, None),
        P("grp"),
        P("grp"),
        P(("grp", "aux"), None, None),
        P(("grp", "aux"), None, None),
    )
    out_specs = P(("grp", "aux"), None, None)
    return jax.shard_map(shards, mesh=mesh, in_specs=in_specs, out_specs=out_specs, check_vma=False)
```

```python
import functools

import jax
import jax.numpy as jnp
from jax import lax
from jax.experimental import pallas as pl
from jax.experimental.pallas import tpu as pltpu
from jax.sharding import PartitionSpec as P

ITERS = 2


def bit_orders(m, descending):
    order0 = list(range(1, m))
    order1 = list(order0)
    if len(order1) >= 2:
        order1[0], order1[1] = order1[1], order1[0]
    if descending:
        return order0[::-1] + [0], order1[::-1] + [0]
    return [0] + order0, [0] + order1


def partners(n, b0, b1):
    return [(d, d ^ (1 << (b1 if d & 1 else b0))) for d in range(n)]


def gather_rows(x, n):
    m = n.bit_length() - 1
    me = lax.axis_index("aux")
    odd = (me & 1) == 1
    order0, order1 = bit_orders(m, True)
    acc = x[None]
    have0, have1 = [], []
    for b0, b1 in zip(order0, order1):
        bit = jnp.where(odd, (me >> b1) & 1, (me >> b0) & 1)
        theirs = lax.ppermute(acc, "aux", partners(n, b0, b1))
        lo = jnp.where(bit == 0, acc, theirs)
        hi = jnp.where(bit == 0, theirs, acc)
        at0 = sum(1 for b in have0 if b > b0)
        at1 = sum(1 for b in have1 if b > b1)
        lead = len(have0)
        lo = lo.reshape((2,) * lead + x.shape) if lead else lo[0]
        hi = hi.reshape((2,) * lead + x.shape) if lead else hi[0]
        new0 = jnp.stack([lo, hi], axis=at0)
        if at1 == at0:
            acc = new0
        else:
            acc = jnp.where(odd, jnp.stack([lo, hi], axis=at1), new0)
        have0 = sorted(have0 + [b0], reverse=True)
        have1 = sorted(have1 + [b1], reverse=True)
        acc = acc.reshape((-1,) + x.shape)
    return acc.reshape((n * x.shape[0],) + x.shape[1:])


def scatter_sum(part, n):
    m = n.bit_length() - 1
    me = lax.axis_index("aux")
    odd = (me & 1) == 1
    rows = part.shape[0] // n
    order0, order1 = bit_orders(m, False)
    acc = part.reshape((2,) * m + (rows,) + part.shape[1:])
    axes0 = list(range(m - 1, -1, -1))
    axes1 = list(axes0)
    for b0, b1 in zip(order0, order1):
        at0, at1 = axes0.index(b0), axes1.index(b1)
        bit0, bit1 = (me >> b0) & 1, (me >> b1) & 1
        if at0 == at1:
            bit = jnp.where(odd, bit1, bit0)
            keep = lax.dynamic_index_in_dim(acc, bit, axis=at0, keepdims=False)
            send = lax.dynamic_index_in_dim(acc, 1 - bit, axis=at0, keepdims=False)
        else:
            keep = jnp.where(
                odd,
                lax.dynamic_index_in_dim(acc, bit1, axis=at1, keepdims=False),
                lax.dynamic_index_in_dim(acc, bit0, axis=at0, keepdims=False),
            )
            send = jnp.where(
                odd,
                lax.dynamic_index_in_dim(acc, 1 - bit1, axis=at1, keepdims=False),
                lax.dynamic_index_in_dim(acc, 1 - bit0, axis=at0, keepdims=False),
            )
        acc = keep + lax.ppermute(send, "aux", partners(n, b0, b1))
        axes0.pop(at0)
        axes1.pop(at1)
    return acc


def exchange_kernel(states, occ_ref, r_ref, vir_ref, out_ref):
    @pl.when(pl.program_id(0) == 0)
    def _():
        out_ref[...] = jnp.zeros_like(out_ref)

    half = jnp.dot(occ_ref[0], r_ref[...], preferred_element_type=jnp.float32).astype(jnp.bfloat16)
    nvir = vir_ref.shape[1]
    vir = vir_ref[0]
    for s in range(states):
        cols = slice(s * nvir, (s + 1) * nvir)
        out_ref[:, cols] += lax.dot_general(
            half[:, cols], vir, (((1,), (1,)), ((), ())), preferred_element_type=jnp.float32
        )


def exchange_part(occ_ints, flat, vir_ints, states):
    local_aux, nocc, _ = occ_ints.shape
    nvir = vir_ints.shape[1]
    width = states * nvir
    return pl.pallas_call(
        functools.partial(exchange_kernel, states),
        grid=(local_aux,),
        in_specs=[
            pl.BlockSpec((1, nocc, nocc), lambda p: (p, 0, 0)),
            pl.BlockSpec((nocc, width), lambda p: (0, 0)),
            pl.BlockSpec((1, nvir, nvir), lambda p: (p, 0, 0)),
        ],
        out_specs=pl.BlockSpec((nocc, width), lambda p: (0, 0)),
        out_shape=jax.ShapeDtypeStruct((nocc, width), jnp.float32),
        compiler_params=pltpu.CompilerParams(dimension_semantics=("arbitrary",)),
    )(occ_ints, flat, vir_ints)


def shards(rhs, occ_energy, vir_energy, occ_ints, vir_ints):
    own_rows = rhs.shape[0]
    states = rhs.shape[1]
    nvir = rhs.shape[2]
    nocc = occ_ints.shape[1]
    n = nocc // own_rows
    assert n & (n - 1) == 0
    position = lax.axis_index("aux")
    my_occ = lax.dynamic_slice_in_dim(occ_energy, position * own_rows, own_rows, 0)
    denom = vir_energy[None, None, :] - my_occ[:, None, None]
    own_denom = denom[:, 0, :]
    resps = [rhs[:, state, :] / own_denom for state in range(states)]
    for step in range(ITERS - 1):
        for state in range(states):
            rounded = resps[state].astype(jnp.bfloat16)
            flat = gather_rows(rounded, n)
            part = exchange_part(occ_ints, flat, vir_ints, 1)
            exchange = scatter_sum(part, n)
            resps[state] = 0.4 * resps[state] + 0.6 * (rhs[:, state, :] - exchange) / own_denom
    response = jnp.stack(resps, axis=1)
    rounded = response.astype(jnp.bfloat16).reshape(own_rows, states * nvir)
    flat = gather_rows(rounded, n)
    part = exchange_part(occ_ints, flat, vir_ints, states)
    exchange = scatter_sum(part, n).reshape(own_rows, states, nvir)
    response = 0.4 * response + 0.6 * (rhs - exchange) / denom
    return response


def solution(mesh):
    in_specs = (
        P(("grp", "aux"), None, None),
        P("grp"),
        P("grp"),
        P(("grp", "aux"), None, None),
        P(("grp", "aux"), None, None),
    )
    out_specs = P(("grp", "aux"), None, None)
    return jax.shard_map(shards, mesh=mesh, in_specs=in_specs, out_specs=out_specs, check_vma=False)
```

```python
import functools

import jax
import jax.numpy as jnp
from jax import lax
from jax.experimental import pallas as pl
from jax.experimental.pallas import tpu as pltpu
from jax.sharding import PartitionSpec as P

ITERS = 2


def bit_orders(m, descending):
    order0 = list(range(1, m))
    order1 = list(order0)
    if len(order1) >= 2:
        order1[0], order1[1] = order1[1], order1[0]
    if descending:
        return order0[::-1] + [0], order1[::-1] + [0]
    return [0] + order0, [0] + order1


def partners(n, b0, b1):
    return [(d, d ^ (1 << (b1 if d & 1 else b0))) for d in range(n)]


def gather_rows(x, n):
    m = n.bit_length() - 1
    me = lax.axis_index("aux")
    odd = (me & 1) == 1
    order0, order1 = bit_orders(m, True)
    acc = x[None]
    have0, have1 = [], []
    for b0, b1 in zip(order0, order1):
        bit = jnp.where(odd, (me >> b1) & 1, (me >> b0) & 1)
        theirs = lax.ppermute(acc, "aux", partners(n, b0, b1))
        lo = jnp.where(bit == 0, acc, theirs)
        hi = jnp.where(bit == 0, theirs, acc)
        at0 = sum(1 for b in have0 if b > b0)
        at1 = sum(1 for b in have1 if b > b1)
        lead = len(have0)
        lo = lo.reshape((2,) * lead + x.shape) if lead else lo[0]
        hi = hi.reshape((2,) * lead + x.shape) if lead else hi[0]
        new0 = jnp.stack([lo, hi], axis=at0)
        if at1 == at0:
            acc = new0
        else:
            acc = jnp.where(odd, jnp.stack([lo, hi], axis=at1), new0)
        have0 = sorted(have0 + [b0], reverse=True)
        have1 = sorted(have1 + [b1], reverse=True)
        acc = acc.reshape((-1,) + x.shape)
    return acc.reshape((n * x.shape[0],) + x.shape[1:])


def scatter_sum(keep, send, n):
    m = n.bit_length() - 1
    me = lax.axis_index("aux")
    odd = (me & 1) == 1
    rows = 2 * keep.shape[0] // n
    order0, order1 = bit_orders(m, False)
    shape = (2,) * (m - 1) + (rows,) + keep.shape[1:]
    acc = keep.reshape(shape) + lax.ppermute(send, "aux", partners(n, 0, 0)).reshape(shape)
    axes0 = list(range(m - 1, 0, -1))
    axes1 = list(axes0)
    for b0, b1 in zip(order0[1:], order1[1:]):
        at0, at1 = axes0.index(b0), axes1.index(b1)
        bit0, bit1 = (me >> b0) & 1, (me >> b1) & 1
        if at0 == at1:
            bit = jnp.where(odd, bit1, bit0)
            kept = lax.dynamic_index_in_dim(acc, bit, axis=at0, keepdims=False)
            sent = lax.dynamic_index_in_dim(acc, 1 - bit, axis=at0, keepdims=False)
        else:
            kept = jnp.where(
                odd,
                lax.dynamic_index_in_dim(acc, bit1, axis=at1, keepdims=False),
                lax.dynamic_index_in_dim(acc, bit0, axis=at0, keepdims=False),
            )
            sent = jnp.where(
                odd,
                lax.dynamic_index_in_dim(acc, 1 - bit1, axis=at1, keepdims=False),
                lax.dynamic_index_in_dim(acc, 1 - bit0, axis=at0, keepdims=False),
            )
        acc = kept + lax.ppermute(sent, "aux", partners(n, b0, b1))
        axes0.pop(at0)
        axes1.pop(at1)
    return acc


def exchange_kernel(states, occ_ref, r_ref, vir_ref, keep_ref, send_ref):
    @pl.when(pl.program_id(0) == 0)
    def _():
        keep_ref[...] = jnp.zeros_like(keep_ref)
        send_ref[...] = jnp.zeros_like(send_ref)

    half = jnp.dot(occ_ref[0], r_ref[...], preferred_element_type=jnp.float32).astype(jnp.bfloat16)
    nvir = vir_ref.shape[1]
    split = keep_ref.shape[0]
    vir = vir_ref[0]
    for s in range(states):
        cols = slice(s * nvir, (s + 1) * nvir)
        term = lax.dot_general(
            half[:, cols], vir, (((1,), (1,)), ((), ())), preferred_element_type=jnp.float32
        )
        keep_ref[:, cols] += term[:split]
        send_ref[:, cols] += term[split:]


def exchange_part(occ_ints, flat, vir_ints, states):
    local_aux, nocc, _ = occ_ints.shape
    nvir = vir_ints.shape[1]
    width = states * nvir
    out = jax.ShapeDtypeStruct((nocc // 2, width), jnp.float32)
    return pl.pallas_call(
        functools.partial(exchange_kernel, states),
        grid=(local_aux,),
        in_specs=[
            pl.BlockSpec((1, nocc, nocc), lambda p: (p, 0, 0)),
            pl.BlockSpec((nocc, width), lambda p: (0, 0)),
            pl.BlockSpec((1, nvir, nvir), lambda p: (p, 0, 0)),
        ],
        out_specs=[
            pl.BlockSpec((nocc // 2, width), lambda p: (0, 0)),
            pl.BlockSpec((nocc // 2, width), lambda p: (0, 0)),
        ],
        out_shape=[out, out],
        compiler_params=pltpu.CompilerParams(dimension_semantics=("arbitrary",)),
    )(occ_ints, flat, vir_ints)


def order_rows(occ_ints, n, core):
    local_aux, nocc, _ = occ_ints.shape
    o = occ_ints.reshape(local_aux, n // 2, 2, nocc // n, nocc)
    even, odd = o[:, :, 0], o[:, :, 1]
    mine = core == 0
    o = jnp.stack([jnp.where(mine, even, odd), jnp.where(mine, odd, even)], axis=1)
    return o.reshape(local_aux, nocc, nocc)


def shards(rhs, occ_energy, vir_energy, occ_ints, vir_ints):
    own_rows = rhs.shape[0]
    states = rhs.shape[1]
    nvir = rhs.shape[2]
    nocc = occ_ints.shape[1]
    n = nocc // own_rows
    assert n & (n - 1) == 0
    position = lax.axis_index("aux")
    my_occ = lax.dynamic_slice_in_dim(occ_energy, position * own_rows, own_rows, 0)
    denom = vir_energy[None, None, :] - my_occ[:, None, None]
    ordered_occ = order_rows(occ_ints, n, position & 1)
    finals = []
    for state in range(states):
        own_rhs = rhs[:, state, :]
        own_denom = denom[:, 0, :]
        resp = own_rhs / own_denom
        for step in range(ITERS):
            rounded = resp.astype(jnp.bfloat16)
            flat = gather_rows(rounded, n)
            keep, send = exchange_part(ordered_occ, flat, vir_ints, 1)
            exchange = scatter_sum(keep, send, n)
            resp = 0.4 * resp + 0.6 * (own_rhs - exchange) / own_denom
        finals.append(resp)
    response = jnp.stack(finals, axis=1)
    return response


def solution(mesh):
    in_specs = (
        P(("grp", "aux"), None, None),
        P("grp"),
        P("grp"),
        P(("grp", "aux"), None, None),
        P(("grp", "aux"), None, None),
    )
    out_specs = P(("grp", "aux"), None, None)
    return jax.shard_map(shards, mesh=mesh, in_specs=in_specs, out_specs=out_specs, check_vma=False)
```

```python
import functools

import jax
import jax.numpy as jnp
from jax import lax
from jax.experimental import pallas as pl
from jax.experimental.pallas import tpu as pltpu
from jax.sharding import PartitionSpec as P

ITERS = 2


def bit_orders(m, descending):
    order0 = list(range(1, m))
    order1 = list(order0)
    if len(order1) >= 2:
        order1[0], order1[1] = order1[1], order1[0]
    if descending:
        return order0[::-1] + [0], order1[::-1] + [0]
    return [0] + order0, [0] + order1


def partners(n, b0, b1):
    return [(d, d ^ (1 << (b1 if d & 1 else b0))) for d in range(n)]


def gather_rows(x, n):
    m = n.bit_length() - 1
    me = lax.axis_index("aux")
    odd = (me & 1) == 1
    order0, order1 = bit_orders(m, True)
    acc = x[None]
    have0, have1 = [], []
    for b0, b1 in zip(order0[:-1], order1[:-1]):
        bit = jnp.where(odd, (me >> b1) & 1, (me >> b0) & 1)
        theirs = lax.ppermute(acc, "aux", partners(n, b0, b1))
        lo = jnp.where(bit == 0, acc, theirs)
        hi = jnp.where(bit == 0, theirs, acc)
        at0 = sum(1 for b in have0 if b > b0)
        at1 = sum(1 for b in have1 if b > b1)
        lead = len(have0)
        lo = lo.reshape((2,) * lead + x.shape) if lead else lo[0]
        hi = hi.reshape((2,) * lead + x.shape) if lead else hi[0]
        new0 = jnp.stack([lo, hi], axis=at0)
        if at1 == at0:
            acc = new0
        else:
            acc = jnp.where(odd, jnp.stack([lo, hi], axis=at1), new0)
        have0 = sorted(have0 + [b0], reverse=True)
        have1 = sorted(have1 + [b1], reverse=True)
        acc = acc.reshape((-1,) + x.shape)
    flat = acc.reshape((n // 2 * x.shape[0],) + x.shape[1:])
    return flat, lax.ppermute(flat, "aux", partners(n, 0, 0))


def scatter_sum(keep, send, n):
    m = n.bit_length() - 1
    me = lax.axis_index("aux")
    odd = (me & 1) == 1
    rows = 2 * keep.shape[0] // n
    order0, order1 = bit_orders(m, False)
    shape = (2,) * (m - 1) + (rows,) + keep.shape[1:]
    acc = keep.reshape(shape) + lax.ppermute(send, "aux", partners(n, 0, 0)).reshape(shape)
    axes0 = list(range(m - 1, 0, -1))
    axes1 = list(axes0)
    for b0, b1 in zip(order0[1:], order1[1:]):
        at0, at1 = axes0.index(b0), axes1.index(b1)
        bit0, bit1 = (me >> b0) & 1, (me >> b1) & 1
        if at0 == at1:
            bit = jnp.where(odd, bit1, bit0)
            kept = lax.dynamic_index_in_dim(acc, bit, axis=at0, keepdims=False)
            sent = lax.dynamic_index_in_dim(acc, 1 - bit, axis=at0, keepdims=False)
        else:
            kept = jnp.where(
                odd,
                lax.dynamic_index_in_dim(acc, bit1, axis=at1, keepdims=False),
                lax.dynamic_index_in_dim(acc, bit0, axis=at0, keepdims=False),
            )
            sent = jnp.where(
                odd,
                lax.dynamic_index_in_dim(acc, 1 - bit1, axis=at1, keepdims=False),
                lax.dynamic_index_in_dim(acc, 1 - bit0, axis=at0, keepdims=False),
            )
        acc = kept + lax.ppermute(sent, "aux", partners(n, b0, b1))
        axes0.pop(at0)
        axes1.pop(at1)
    return acc


def exchange_kernel(states, occ_ref, mine_ref, theirs_ref, vir_ref, keep_ref, send_ref, r_ref):
    @pl.when(pl.program_id(0) == 0)
    def _():
        keep_ref[...] = jnp.zeros_like(keep_ref)
        send_ref[...] = jnp.zeros_like(send_ref)
        split = mine_ref.shape[0]
        r_ref[:split] = mine_ref[...]
        r_ref[split:] = theirs_ref[...]

    half = jnp.dot(occ_ref[0], r_ref[...], preferred_element_type=jnp.float32).astype(jnp.bfloat16)
    nvir = vir_ref.shape[1]
    split = keep_ref.shape[0]
    vir = vir_ref[0]
    for s in range(states):
        cols = slice(s * nvir, (s + 1) * nvir)
        term = lax.dot_general(
            half[:, cols], vir, (((1,), (1,)), ((), ())), preferred_element_type=jnp.float32
        )
        keep_ref[:, cols] += term[:split]
        send_ref[:, cols] += term[split:]


def exchange_part(occ_ints, mine, theirs, vir_ints, states):
    local_aux, nocc, _ = occ_ints.shape
    nvir = vir_ints.shape[1]
    width = states * nvir
    out = jax.ShapeDtypeStruct((nocc // 2, width), jnp.float32)
    return pl.pallas_call(
        functools.partial(exchange_kernel, states),
        grid=(local_aux,),
        in_specs=[
            pl.BlockSpec((1, nocc, nocc), lambda p: (p, 0, 0)),
            pl.BlockSpec((nocc // 2, width), lambda p: (0, 0)),
            pl.BlockSpec((nocc // 2, width), lambda p: (0, 0)),
            pl.BlockSpec((1, nvir, nvir), lambda p: (p, 0, 0)),
        ],
        out_specs=[
            pl.BlockSpec((nocc // 2, width), lambda p: (0, 0)),
            pl.BlockSpec((nocc // 2, width), lambda p: (0, 0)),
        ],
        out_shape=[out, out],
        scratch_shapes=[pltpu.VMEM((nocc, width), jnp.bfloat16)],
        compiler_params=pltpu.CompilerParams(dimension_semantics=("arbitrary",)),
    )(occ_ints, mine, theirs, vir_ints)


def order_columns(occ_ints, n, core):
    local_aux, nocc, _ = occ_ints.shape
    rows = nocc // n
    dest = jnp.arange(nocc)
    block, within = dest // rows, dest % rows
    upper = block // (n // 2)
    source = ((block % (n // 2)) * 2 + (upper ^ core)) * rows + within
    select = (jnp.arange(nocc)[:, None] == source[None, :]).astype(occ_ints.dtype)
    moved = jnp.dot(occ_ints.reshape(local_aux * nocc, nocc), select, preferred_element_type=jnp.float32)
    return moved.astype(occ_ints.dtype).reshape(local_aux, nocc, nocc)


def order_rows(occ_ints, n, core):
    local_aux, nocc, _ = occ_ints.shape
    o = occ_ints.reshape(local_aux, n // 2, 2, nocc // n, nocc)
    even, odd = o[:, :, 0], o[:, :, 1]
    mine = core == 0
    o = jnp.stack([jnp.where(mine, even, odd), jnp.where(mine, odd, even)], axis=1)
    return o.reshape(local_aux, nocc, nocc)


def shards(rhs, occ_energy, vir_energy, occ_ints, vir_ints):
    own_rows = rhs.shape[0]
    states = rhs.shape[1]
    nvir = rhs.shape[2]
    nocc = occ_ints.shape[1]
    n = nocc // own_rows
    assert n & (n - 1) == 0
    position = lax.axis_index("aux")
    my_occ = lax.dynamic_slice_in_dim(occ_energy, position * own_rows, own_rows, 0)
    denom = vir_energy[None, None, :] - my_occ[:, None, None]
    ordered_occ = order_columns(order_rows(occ_ints, n, position & 1), n, position & 1)
    finals = []
    for state in range(states):
        own_rhs = rhs[:, state, :]
        own_denom = denom[:, 0, :]
        resp = own_rhs / own_denom
        for step in range(ITERS):
            rounded = resp.astype(jnp.bfloat16)
            mine, theirs = gather_rows(rounded, n)
            keep, send = exchange_part(ordered_occ, mine, theirs, vir_ints, 1)
            exchange = scatter_sum(keep, send, n)
            resp = 0.4 * resp + 0.6 * (own_rhs - exchange) / own_denom
        finals.append(resp)
    response = jnp.stack(finals, axis=1)
    return response


def solution(mesh):
    in_specs = (
        P(("grp", "aux"), None, None),
        P("grp"),
        P("grp"),
        P(("grp", "aux"), None, None),
        P(("grp", "aux"), None, None),
    )
    out_specs = P(("grp", "aux"), None, None)
    return jax.shard_map(shards, mesh=mesh, in_specs=in_specs, out_specs=out_specs, check_vma=False)
```

```python
import functools

import jax
import jax.numpy as jnp
from jax import lax
from jax.experimental import pallas as pl
from jax.experimental.pallas import tpu as pltpu
from jax.sharding import PartitionSpec as P

ITERS = 2
PIECES = 2


def bit_orders(m, descending):
    order0 = list(range(1, m))
    order1 = list(order0)
    if len(order1) >= 2:
        order1[0], order1[1] = order1[1], order1[0]
    if descending:
        return order0[::-1] + [0], order1[::-1] + [0]
    return [0] + order0, [0] + order1


def partners(n, b0, b1):
    return [(d, d ^ (1 << (b1 if d & 1 else b0))) for d in range(n)]


def gather_rows(x, n):
    m = n.bit_length() - 1
    me = lax.axis_index("aux")
    odd = (me & 1) == 1
    order0, order1 = bit_orders(m, True)
    acc = x[None]
    have0, have1 = [], []
    for b0, b1 in zip(order0[:-1], order1[:-1]):
        bit = jnp.where(odd, (me >> b1) & 1, (me >> b0) & 1)
        theirs = lax.ppermute(acc, "aux", partners(n, b0, b1))
        lo = jnp.where(bit == 0, acc, theirs)
        hi = jnp.where(bit == 0, theirs, acc)
        at0 = sum(1 for b in have0 if b > b0)
        at1 = sum(1 for b in have1 if b > b1)
        lead = len(have0)
        lo = lo.reshape((2,) * lead + x.shape) if lead else lo[0]
        hi = hi.reshape((2,) * lead + x.shape) if lead else hi[0]
        new0 = jnp.stack([lo, hi], axis=at0)
        if at1 == at0:
            acc = new0
        else:
            acc = jnp.where(odd, jnp.stack([lo, hi], axis=at1), new0)
        have0 = sorted(have0 + [b0], reverse=True)
        have1 = sorted(have1 + [b1], reverse=True)
        acc = acc.reshape((-1,) + x.shape)
    flat = acc.reshape((n // 2 * x.shape[0],) + x.shape[1:])
    return flat, lax.ppermute(flat, "aux", partners(n, 0, 0))


def scatter_sum(keep, send, n):
    m = n.bit_length() - 1
    me = lax.axis_index("aux")
    odd = (me & 1) == 1
    rows = 2 * keep.shape[0] // n
    order0, order1 = bit_orders(m, False)
    shape = (2,) * (m - 1) + (rows,) + keep.shape[1:]
    acc = keep.reshape(shape) + lax.ppermute(send, "aux", partners(n, 0, 0)).reshape(shape)
    axes0 = list(range(m - 1, 0, -1))
    axes1 = list(axes0)
    for b0, b1 in zip(order0[1:], order1[1:]):
        at0, at1 = axes0.index(b0), axes1.index(b1)
        bit0, bit1 = (me >> b0) & 1, (me >> b1) & 1
        if at0 == at1:
            bit = jnp.where(odd, bit1, bit0)
            kept = lax.dynamic_index_in_dim(acc, bit, axis=at0, keepdims=False)
            sent = lax.dynamic_index_in_dim(acc, 1 - bit, axis=at0, keepdims=False)
        else:
            kept = jnp.where(
                odd,
                lax.dynamic_index_in_dim(acc, bit1, axis=at1, keepdims=False),
                lax.dynamic_index_in_dim(acc, bit0, axis=at0, keepdims=False),
            )
            sent = jnp.where(
                odd,
                lax.dynamic_index_in_dim(acc, 1 - bit1, axis=at1, keepdims=False),
                lax.dynamic_index_in_dim(acc, 1 - bit0, axis=at0, keepdims=False),
            )
        acc = kept + lax.ppermute(sent, "aux", partners(n, b0, b1))
        axes0.pop(at0)
        axes1.pop(at1)
    return acc


def exchange_kernel(states, pieces, occ_ref, *refs):
    mine, theirs = refs[:pieces], refs[pieces:2 * pieces]
    vir_ref = refs[2 * pieces]
    keep, send = refs[2 * pieces + 1:3 * pieces + 1], refs[3 * pieces + 1:4 * pieces + 1]
    r_ref = refs[4 * pieces + 1]
    split = mine[0].shape[0]
    width = mine[0].shape[1]

    @pl.when(pl.program_id(0) == 0)
    def _():
        for q in range(pieces):
            keep[q][...] = jnp.zeros_like(keep[q])
            send[q][...] = jnp.zeros_like(send[q])
            r_ref[:split, q * width:(q + 1) * width] = mine[q][...]
            r_ref[split:, q * width:(q + 1) * width] = theirs[q][...]

    half = jnp.dot(occ_ref[0], r_ref[...], preferred_element_type=jnp.float32).astype(jnp.bfloat16)
    vir = vir_ref[0]
    term = lax.dot_general(half, vir, (((1,), (1,)), ((), ())), preferred_element_type=jnp.float32)
    for q in range(pieces):
        keep[q][...] += term[:split, q * width:(q + 1) * width]
        send[q][...] += term[split:, q * width:(q + 1) * width]


def exchange_part(occ_ints, mine, theirs, vir_ints):
    local_aux, nocc, _ = occ_ints.shape
    nvir = vir_ints.shape[1]
    pieces = len(mine)
    width = nvir // pieces
    piece = pl.BlockSpec((nocc // 2, width), lambda p: (0, 0))
    out = jax.ShapeDtypeStruct((nocc // 2, width), jnp.float32)
    results = pl.pallas_call(
        functools.partial(exchange_kernel, 1, pieces),
        grid=(local_aux,),
        in_specs=[pl.BlockSpec((1, nocc, nocc), lambda p: (p, 0, 0))]
        + [piece] * (2 * pieces)
        + [pl.BlockSpec((1, nvir, nvir), lambda p: (p, 0, 0))],
        out_specs=[piece] * (2 * pieces),
        out_shape=[out] * (2 * pieces),
        scratch_shapes=[pltpu.VMEM((nocc, nvir), jnp.bfloat16)],
        compiler_params=pltpu.CompilerParams(dimension_semantics=("arbitrary",)),
    )(occ_ints, *mine, *theirs, vir_ints)
    return results[:pieces], results[pieces:]


def order_columns(occ_ints, n, core):
    local_aux, nocc, _ = occ_ints.shape
    rows = nocc // n
    dest = jnp.arange(nocc)
    block, within = dest // rows, dest % rows
    upper = block // (n // 2)
    source = ((block % (n // 2)) * 2 + (upper ^ core)) * rows + within
    select = (jnp.arange(nocc)[:, None] == source[None, :]).astype(occ_ints.dtype)
    moved = jnp.dot(occ_ints.reshape(local_aux * nocc, nocc), select, preferred_element_type=jnp.float32)
    return moved.astype(occ_ints.dtype).reshape(local_aux, nocc, nocc)


def order_rows(occ_ints, n, core):
    local_aux, nocc, _ = occ_ints.shape
    o = occ_ints.reshape(local_aux, n // 2, 2, nocc // n, nocc)
    even, odd = o[:, :, 0], o[:, :, 1]
    mine = core == 0
    o = jnp.stack([jnp.where(mine, even, odd), jnp.where(mine, odd, even)], axis=1)
    return o.reshape(local_aux, nocc, nocc)


def shards(rhs, occ_energy, vir_energy, occ_ints, vir_ints):
    own_rows = rhs.shape[0]
    states = rhs.shape[1]
    nvir = rhs.shape[2]
    nocc = occ_ints.shape[1]
    n = nocc // own_rows
    assert n & (n - 1) == 0
    position = lax.axis_index("aux")
    my_occ = lax.dynamic_slice_in_dim(occ_energy, position * own_rows, own_rows, 0)
    denom = vir_energy[None, None, :] - my_occ[:, None, None]
    ordered_occ = order_columns(order_rows(occ_ints, n, position & 1), n, position & 1)
    finals = []
    for state in range(states):
        own_rhs = rhs[:, state, :]
        own_denom = denom[:, 0, :]
        resp = own_rhs / own_denom
        for step in range(ITERS):
            rounded = resp.astype(jnp.bfloat16)
            width = nvir // PIECES
            got = [gather_rows(rounded[:, q * width:(q + 1) * width], n) for q in range(PIECES)]
            keep, send = exchange_part(ordered_occ, [g[0] for g in got], [g[1] for g in got], vir_ints)
            exchange = jnp.concatenate([scatter_sum(k, t, n) for k, t in zip(keep, send)], axis=1)
            resp = 0.4 * resp + 0.6 * (own_rhs - exchange) / own_denom
        finals.append(resp)
    response = jnp.stack(finals, axis=1)
    return response


def solution(mesh):
    in_specs = (
        P(("grp", "aux"), None, None),
        P("grp"),
        P("grp"),
        P(("grp", "aux"), None, None),
        P(("grp", "aux"), None, None),
    )
    out_specs = P(("grp", "aux"), None, None)
    return jax.shard_map(shards, mesh=mesh, in_specs=in_specs, out_specs=out_specs, check_vma=False)
```

```python
import functools

import jax
import jax.numpy as jnp
from jax import lax
from jax.experimental import pallas as pl
from jax.experimental.pallas import tpu as pltpu
from jax.sharding import PartitionSpec as P

ITERS = 2


def bit_orders(m, descending):
    order0 = list(range(1, m))
    order1 = list(order0)
    if len(order1) >= 2:
        order1[0], order1[1] = order1[1], order1[0]
    if descending:
        return order0[::-1] + [0], order1[::-1] + [0]
    return [0] + order0, [0] + order1


def partners(n, b0, b1):
    return [(d, d ^ (1 << (b1 if d & 1 else b0))) for d in range(n)]


def gather_rows(x, n):
    m = n.bit_length() - 1
    me = lax.axis_index("aux")
    odd = (me & 1) == 1
    order0, order1 = bit_orders(m, True)
    acc = x[None]
    have0, have1 = [], []
    for b0, b1 in zip(order0[:-1], order1[:-1]):
        bit = jnp.where(odd, (me >> b1) & 1, (me >> b0) & 1)
        theirs = lax.ppermute(acc, "aux", partners(n, b0, b1))
        lo = jnp.where(bit == 0, acc, theirs)
        hi = jnp.where(bit == 0, theirs, acc)
        at0 = sum(1 for b in have0 if b > b0)
        at1 = sum(1 for b in have1 if b > b1)
        lead = len(have0)
        lo = lo.reshape((2,) * lead + x.shape) if lead else lo[0]
        hi = hi.reshape((2,) * lead + x.shape) if lead else hi[0]
        new0 = jnp.stack([lo, hi], axis=at0)
        if at1 == at0:
            acc = new0
        else:
            acc = jnp.where(odd, jnp.stack([lo, hi], axis=at1), new0)
        have0 = sorted(have0 + [b0], reverse=True)
        have1 = sorted(have1 + [b1], reverse=True)
        acc = acc.reshape((-1,) + x.shape)
    flat = acc.reshape((n // 2 * x.shape[0],) + x.shape[1:])
    return flat, lax.ppermute(flat, "aux", partners(n, 0, 0))


def scatter_sum(keep, send, n):
    m = n.bit_length() - 1
    me = lax.axis_index("aux")
    odd = (me & 1) == 1
    rows = 2 * keep.shape[0] // n
    order0, order1 = bit_orders(m, False)
    shape = (2,) * (m - 1) + (rows,) + keep.shape[1:]
    acc = keep.reshape(shape) + lax.ppermute(send, "aux", partners(n, 0, 0)).reshape(shape)
    axes0 = list(range(m - 1, 0, -1))
    axes1 = list(axes0)
    for b0, b1 in zip(order0[1:], order1[1:]):
        at0, at1 = axes0.index(b0), axes1.index(b1)
        bit0, bit1 = (me >> b0) & 1, (me >> b1) & 1
        if at0 == at1:
            bit = jnp.where(odd, bit1, bit0)
            kept = lax.dynamic_index_in_dim(acc, bit, axis=at0, keepdims=False)
            sent = lax.dynamic_index_in_dim(acc, 1 - bit, axis=at0, keepdims=False)
        else:
            kept = jnp.where(
                odd,
                lax.dynamic_index_in_dim(acc, bit1, axis=at1, keepdims=False),
                lax.dynamic_index_in_dim(acc, bit0, axis=at0, keepdims=False),
            )
            sent = jnp.where(
                odd,
                lax.dynamic_index_in_dim(acc, 1 - bit1, axis=at1, keepdims=False),
                lax.dynamic_index_in_dim(acc, 1 - bit0, axis=at0, keepdims=False),
            )
        acc = kept + lax.ppermute(sent, "aux", partners(n, b0, b1))
        axes0.pop(at0)
        axes1.pop(at1)
    return acc


def exchange_kernel(states, occ_ref, *refs):
    mine, theirs = refs[:states], refs[states:2 * states]
    vir_ref = refs[2 * states]
    keep, send = refs[2 * states + 1:3 * states + 1], refs[3 * states + 1:4 * states + 1]
    r_ref = refs[4 * states + 1]
    split = mine[0].shape[0]
    nvir = vir_ref.shape[1]

    @pl.when(pl.program_id(0) == 0)
    def _():
        for s in range(states):
            keep[s][...] = jnp.zeros_like(keep[s])
            send[s][...] = jnp.zeros_like(send[s])
            r_ref[:split, s * nvir:(s + 1) * nvir] = mine[s][...]
            r_ref[split:, s * nvir:(s + 1) * nvir] = theirs[s][...]

    half = jnp.dot(occ_ref[0], r_ref[...], preferred_element_type=jnp.float32).astype(jnp.bfloat16)
    vir = vir_ref[0]
    for s in range(states):
        term = lax.dot_general(
            half[:, s * nvir:(s + 1) * nvir], vir, (((1,), (1,)), ((), ())), preferred_element_type=jnp.float32
        )
        keep[s][...] += term[:split]
        send[s][...] += term[split:]


def exchange_part(occ_ints, mine, theirs, vir_ints):
    local_aux, nocc, _ = occ_ints.shape
    nvir = vir_ints.shape[1]
    states = len(mine)
    piece = pl.BlockSpec((nocc // 2, nvir), lambda p: (0, 0))
    out = jax.ShapeDtypeStruct((nocc // 2, nvir), jnp.float32)
    results = pl.pallas_call(
        functools.partial(exchange_kernel, states),
        grid=(local_aux,),
        in_specs=[pl.BlockSpec((1, nocc, nocc), lambda p: (p, 0, 0))]
        + [piece] * (2 * states)
        + [pl.BlockSpec((1, nvir, nvir), lambda p: (p, 0, 0))],
        out_specs=[piece] * (2 * states),
        out_shape=[out] * (2 * states),
        scratch_shapes=[pltpu.VMEM((nocc, states * nvir), jnp.bfloat16)],
        compiler_params=pltpu.CompilerParams(dimension_semantics=("arbitrary",)),
    )(occ_ints, *mine, *theirs, vir_ints)
    return results[:states], results[states:]


def order_columns(occ_ints, n, core):
    local_aux, nocc, _ = occ_ints.shape
    rows = nocc // n
    dest = jnp.arange(nocc)
    block, within = dest // rows, dest % rows
    upper = block // (n // 2)
    source = ((block % (n // 2)) * 2 + (upper ^ core)) * rows + within
    select = (jnp.arange(nocc)[:, None] == source[None, :]).astype(occ_ints.dtype)
    moved = jnp.dot(occ_ints.reshape(local_aux * nocc, nocc), select, preferred_element_type=jnp.float32)
    return moved.astype(occ_ints.dtype).reshape(local_aux, nocc, nocc)


def order_rows(occ_ints, n, core):
    local_aux, nocc, _ = occ_ints.shape
    o = occ_ints.reshape(local_aux, n // 2, 2, nocc // n, nocc)
    even, odd = o[:, :, 0], o[:, :, 1]
    mine = core == 0
    o = jnp.stack([jnp.where(mine, even, odd), jnp.where(mine, odd, even)], axis=1)
    return o.reshape(local_aux, nocc, nocc)


def shards(rhs, occ_energy, vir_energy, occ_ints, vir_ints):
    own_rows = rhs.shape[0]
    states = rhs.shape[1]
    nvir = rhs.shape[2]
    nocc = occ_ints.shape[1]
    n = nocc // own_rows
    assert n & (n - 1) == 0
    position = lax.axis_index("aux")
    my_occ = lax.dynamic_slice_in_dim(occ_energy, position * own_rows, own_rows, 0)
    denom = vir_energy[None, None, :] - my_occ[:, None, None]
    ordered_occ = order_columns(order_rows(occ_ints, n, position & 1), n, position & 1)
    own_denom = denom[:, 0, :]
    resps = [rhs[:, state, :] / own_denom for state in range(states)]
    for step in range(ITERS):
        got = [gather_rows(resp.astype(jnp.bfloat16), n) for resp in resps]
        keep, send = exchange_part(ordered_occ, [g[0] for g in got], [g[1] for g in got], vir_ints)
        for state in range(states):
            exchange = scatter_sum(keep[state], send[state], n)
            resps[state] = 0.4 * resps[state] + 0.6 * (rhs[:, state, :] - exchange) / own_denom
    response = jnp.stack(resps, axis=1)
    return response


def solution(mesh):
    in_specs = (
        P(("grp", "aux"), None, None),
        P("grp"),
        P("grp"),
        P(("grp", "aux"), None, None),
        P(("grp", "aux"), None, None),
    )
    out_specs = P(("grp", "aux"), None, None)
    return jax.shard_map(shards, mesh=mesh, in_specs=in_specs, out_specs=out_specs, check_vma=False)
```

```python
import functools

import jax
import jax.numpy as jnp
from jax import lax
from jax.experimental import pallas as pl
from jax.experimental.pallas import tpu as pltpu
from jax.sharding import PartitionSpec as P

ITERS = 2


def bit_orders(m, descending):
    order0 = list(range(1, m))
    order1 = list(order0)
    if len(order1) >= 2:
        order1[0], order1[1] = order1[1], order1[0]
    if descending:
        return order0[::-1] + [0], order1[::-1] + [0]
    return [0] + order0, [0] + order1


def partners(n, b0, b1):
    return [(d, d ^ (1 << (b1 if d & 1 else b0))) for d in range(n)]


def gather_rows(x, n):
    m = n.bit_length() - 1
    me = lax.axis_index("aux")
    odd = (me & 1) == 1
    order0, order1 = bit_orders(m, True)
    acc = x[None]
    have0, have1 = [], []
    for b0, b1 in zip(order0[:-1], order1[:-1]):
        bit = jnp.where(odd, (me >> b1) & 1, (me >> b0) & 1)
        theirs = lax.ppermute(acc, "aux", partners(n, b0, b1))
        lo = jnp.where(bit == 0, acc, theirs)
        hi = jnp.where(bit == 0, theirs, acc)
        at0 = sum(1 for b in have0 if b > b0)
        at1 = sum(1 for b in have1 if b > b1)
        lead = len(have0)
        lo = lo.reshape((2,) * lead + x.shape) if lead else lo[0]
        hi = hi.reshape((2,) * lead + x.shape) if lead else hi[0]
        new0 = jnp.stack([lo, hi], axis=at0)
        if at1 == at0:
            acc = new0
        else:
            acc = jnp.where(odd, jnp.stack([lo, hi], axis=at1), new0)
        have0 = sorted(have0 + [b0], reverse=True)
        have1 = sorted(have1 + [b1], reverse=True)
        acc = acc.reshape((-1,) + x.shape)
    flat = acc.reshape((n // 2 * x.shape[0],) + x.shape[1:])
    return flat, lax.ppermute(flat, "aux", partners(n, 0, 0))


def scatter_sum(keep, send, n):
    m = n.bit_length() - 1
    me = lax.axis_index("aux")
    odd = (me & 1) == 1
    rows = 2 * keep.shape[0] // n
    order0, order1 = bit_orders(m, False)
    shape = (2,) * (m - 1) + (rows,) + keep.shape[1:]
    parts = [keep.reshape(shape), lax.ppermute(send, "aux", partners(n, 0, 0)).reshape(shape)]
    axes0 = list(range(m - 1, 0, -1))
    axes1 = list(axes0)
    for b0, b1 in zip(order0[1:], order1[1:]):
        at0, at1 = axes0.index(b0), axes1.index(b1)
        bit0, bit1 = (me >> b0) & 1, (me >> b1) & 1

        def pick(choice):
            total = 0.0
            for piece in parts:
                if at0 == at1:
                    bit = jnp.where(odd, bit1, bit0)
                    got = lax.dynamic_index_in_dim(piece, bit ^ choice, axis=at0, keepdims=False)
                else:
                    got = jnp.where(
                        odd,
                        lax.dynamic_index_in_dim(piece, bit1 ^ choice, axis=at1, keepdims=False),
                        lax.dynamic_index_in_dim(piece, bit0 ^ choice, axis=at0, keepdims=False),
                    )
                total = total + got
            return total

        kept, sent = pick(0), pick(1)
        parts = [kept + lax.ppermute(sent, "aux", partners(n, b0, b1))]
        axes0.pop(at0)
        axes1.pop(at1)
    acc = sum(parts[1:], parts[0])
    return acc


def exchange_kernel(states, occ_ref, *refs):
    mine, theirs = refs[:states], refs[states:2 * states]
    vir_ref = refs[2 * states]
    keep, send = refs[2 * states + 1:3 * states + 1], refs[3 * states + 1:4 * states + 1]
    r_ref = refs[4 * states + 1]
    split = mine[0].shape[0]
    nvir = vir_ref.shape[1]

    @pl.when(pl.program_id(0) == 0)
    def _():
        for s in range(states):
            keep[s][...] = jnp.zeros_like(keep[s])
            send[s][...] = jnp.zeros_like(send[s])
            r_ref[:split, s * nvir:(s + 1) * nvir] = mine[s][...]
            r_ref[split:, s * nvir:(s + 1) * nvir] = theirs[s][...]

    half = jnp.dot(occ_ref[0], r_ref[...], preferred_element_type=jnp.float32).astype(jnp.bfloat16)
    vir = vir_ref[0]
    for s in range(states):
        term = lax.dot_general(
            half[:, s * nvir:(s + 1) * nvir], vir, (((1,), (1,)), ((), ())), preferred_element_type=jnp.float32
        )
        keep[s][...] += term[:split]
        send[s][...] += term[split:]


def exchange_part(occ_ints, mine, theirs, vir_ints):
    local_aux, nocc, _ = occ_ints.shape
    nvir = vir_ints.shape[1]
    states = len(mine)
    piece = pl.BlockSpec((nocc // 2, nvir), lambda p: (0, 0))
    out = jax.ShapeDtypeStruct((nocc // 2, nvir), jnp.float32)
    results = pl.pallas_call(
        functools.partial(exchange_kernel, states),
        grid=(local_aux,),
        in_specs=[pl.BlockSpec((1, nocc, nocc), lambda p: (p, 0, 0))]
        + [piece] * (2 * states)
        + [pl.BlockSpec((1, nvir, nvir), lambda p: (p, 0, 0))],
        out_specs=[piece] * (2 * states),
        out_shape=[out] * (2 * states),
        scratch_shapes=[pltpu.VMEM((nocc, states * nvir), jnp.bfloat16)],
        compiler_params=pltpu.CompilerParams(dimension_semantics=("arbitrary",)),
    )(occ_ints, *mine, *theirs, vir_ints)
    return results[:states], results[states:]


def order_columns(occ_ints, n, core):
    local_aux, nocc, _ = occ_ints.shape
    rows = nocc // n
    dest = jnp.arange(nocc)
    block, within = dest // rows, dest % rows
    upper = block // (n // 2)
    source = ((block % (n // 2)) * 2 + (upper ^ core)) * rows + within
    select = (jnp.arange(nocc)[:, None] == source[None, :]).astype(occ_ints.dtype)
    moved = jnp.dot(occ_ints.reshape(local_aux * nocc, nocc), select, preferred_element_type=jnp.float32)
    return moved.astype(occ_ints.dtype).reshape(local_aux, nocc, nocc)


def order_rows(occ_ints, n, core):
    local_aux, nocc, _ = occ_ints.shape
    o = occ_ints.reshape(local_aux, n // 2, 2, nocc // n, nocc)
    even, odd = o[:, :, 0], o[:, :, 1]
    mine = core == 0
    o = jnp.stack([jnp.where(mine, even, odd), jnp.where(mine, odd, even)], axis=1)
    return o.reshape(local_aux, nocc, nocc)


def shards(rhs, occ_energy, vir_energy, occ_ints, vir_ints):
    own_rows = rhs.shape[0]
    states = rhs.shape[1]
    nvir = rhs.shape[2]
    nocc = occ_ints.shape[1]
    n = nocc // own_rows
    assert n & (n - 1) == 0
    position = lax.axis_index("aux")
    wanted = position * own_rows + jnp.arange(own_rows)
    my_occ = jnp.sum(jnp.where(jnp.arange(nocc)[None, :] == wanted[:, None], occ_energy[None, :], 0.0), axis=1)
    denom = vir_energy[None, None, :] - my_occ[:, None, None]
    ordered_occ = order_columns(order_rows(occ_ints, n, position & 1), n, position & 1)
    own_denom = denom[:, 0, :]
    resps = [rhs[:, state, :] / own_denom for state in range(states)]
    for step in range(ITERS):
        got = [gather_rows(resp.astype(jnp.bfloat16), n) for resp in resps]
        keep, send = exchange_part(ordered_occ, [g[0] for g in got], [g[1] for g in got], vir_ints)
        for state in range(states):
            exchange = scatter_sum(keep[state], send[state], n)
            resps[state] = 0.4 * resps[state] + 0.6 * (rhs[:, state, :] - exchange) / own_denom
    response = jnp.stack(resps, axis=1)
    return response


def solution(mesh):
    in_specs = (
        P(("grp", "aux"), None, None),
        P("grp"),
        P("grp"),
        P(("grp", "aux"), None, None),
        P(("grp", "aux"), None, None),
    )
    out_specs = P(("grp", "aux"), None, None)
    return jax.shard_map(shards, mesh=mesh, in_specs=in_specs, out_specs=out_specs, check_vma=False)
```

```python
import functools

import jax
import jax.numpy as jnp
from jax import lax
from jax.experimental import pallas as pl
from jax.experimental.pallas import tpu as pltpu
from jax.sharding import PartitionSpec as P

ITERS = 2
JOINT = 2


def bit_orders(m, descending):
    order0 = list(range(1, m))
    order1 = list(order0)
    if len(order1) >= 2:
        order1[0], order1[1] = order1[1], order1[0]
    if descending:
        return order0[::-1] + [0], order1[::-1] + [0]
    return [0] + order0, [0] + order1


def partners(n, b0, b1):
    return [(d, d ^ (1 << (b1 if d & 1 else b0))) for d in range(n)]


def gather_step(acc, item, have0, have1, b0, b1, n, me, odd):
    bit = jnp.where(odd, (me >> b1) & 1, (me >> b0) & 1)
    theirs = lax.ppermute(acc, "aux", partners(n, b0, b1))
    lo = jnp.where(bit == 0, acc, theirs)
    hi = jnp.where(bit == 0, theirs, acc)
    at0 = sum(1 for b in have0 if b > b0)
    at1 = sum(1 for b in have1 if b > b1)
    lead = len(have0)
    lo = lo.reshape((2,) * lead + item) if lead else lo[0]
    hi = hi.reshape((2,) * lead + item) if lead else hi[0]
    new0 = jnp.stack([lo, hi], axis=at0)
    acc = new0 if at1 == at0 else jnp.where(odd, jnp.stack([lo, hi], axis=at1), new0)
    return acc.reshape((-1,) + item), sorted(have0 + [b0], reverse=True), sorted(have1 + [b1], reverse=True)


def gather_rows(xs, n, joint):
    m = n.bit_length() - 1
    me = lax.axis_index("aux")
    odd = (me & 1) == 1
    order0, order1 = bit_orders(m, True)
    steps = list(zip(order0[:-1], order1[:-1]))
    item = (len(xs),) + xs[0].shape
    acc = jnp.stack(xs)[None]
    have0, have1 = [], []
    for b0, b1 in steps[:joint]:
        acc, have0, have1 = gather_step(acc, item, have0, have1, b0, b1, n, me, odd)
    result = []
    for state in range(len(xs)):
        own = acc[:, state]
        h0, h1 = have0, have1
        for b0, b1 in steps[joint:]:
            own, h0, h1 = gather_step(own, xs[0].shape, h0, h1, b0, b1, n, me, odd)
        flat = own.reshape((n // 2 * xs[0].shape[0],) + xs[0].shape[1:])
        result.append((flat, lax.ppermute(flat, "aux", partners(n, 0, 0))))
    return result


def reduce_step(acc, axes0, axes1, b0, b1, n, me, odd):
    at0, at1 = axes0.index(b0), axes1.index(b1)
    bit0, bit1 = (me >> b0) & 1, (me >> b1) & 1
    if at0 == at1:
        bit = jnp.where(odd, bit1, bit0)
        kept = lax.dynamic_index_in_dim(acc, bit, axis=at0, keepdims=False)
        sent = lax.dynamic_index_in_dim(acc, 1 - bit, axis=at0, keepdims=False)
    else:
        kept = jnp.where(
            odd,
            lax.dynamic_index_in_dim(acc, bit1, axis=at1, keepdims=False),
            lax.dynamic_index_in_dim(acc, bit0, axis=at0, keepdims=False),
        )
        sent = jnp.where(
            odd,
            lax.dynamic_index_in_dim(acc, 1 - bit1, axis=at1, keepdims=False),
            lax.dynamic_index_in_dim(acc, 1 - bit0, axis=at0, keepdims=False),
        )
    acc = kept + lax.ppermute(sent, "aux", partners(n, b0, b1))
    return acc, axes0[:at0] + axes0[at0 + 1:], axes1[:at1] + axes1[at1 + 1:]


def scatter_sum(keeps, sends, n, joint):
    m = n.bit_length() - 1
    me = lax.axis_index("aux")
    odd = (me & 1) == 1
    rows = 2 * keeps[0].shape[0] // n
    order0, order1 = bit_orders(m, False)
    steps = list(zip(order0[1:], order1[1:]))
    split = len(steps) - joint
    shape = (2,) * (m - 1) + (rows,) + keeps[0].shape[1:]
    accs = []
    for keep, send in zip(keeps, sends):
        acc = keep.reshape(shape) + lax.ppermute(send, "aux", partners(n, 0, 0)).reshape(shape)
        axes0 = list(range(m - 1, 0, -1))
        axes1 = list(axes0)
        for b0, b1 in steps[:split]:
            acc, axes0, axes1 = reduce_step(acc, axes0, axes1, b0, b1, n, me, odd)
        accs.append(acc)
    acc = jnp.stack(accs, axis=len(axes0))
    for b0, b1 in steps[split:]:
        acc, axes0, axes1 = reduce_step(acc, axes0, axes1, b0, b1, n, me, odd)
    return [acc[state] for state in range(len(keeps))]


def exchange_kernel(states, occ_ref, *refs):
    mine, theirs = refs[:states], refs[states:2 * states]
    vir_ref = refs[2 * states]
    keep, send = refs[2 * states + 1:3 * states + 1], refs[3 * states + 1:4 * states + 1]
    r_ref = refs[4 * states + 1]
    split = mine[0].shape[0]
    nvir = vir_ref.shape[1]

    @pl.when(pl.program_id(0) == 0)
    def _():
        for s in range(states):
            keep[s][...] = jnp.zeros_like(keep[s])
            send[s][...] = jnp.zeros_like(send[s])
            r_ref[:split, s * nvir:(s + 1) * nvir] = mine[s][...]
            r_ref[split:, s * nvir:(s + 1) * nvir] = theirs[s][...]

    half = jnp.dot(occ_ref[0], r_ref[...], preferred_element_type=jnp.float32).astype(jnp.bfloat16)
    vir = vir_ref[0]
    for s in range(states):
        term = lax.dot_general(
            half[:, s * nvir:(s + 1) * nvir], vir, (((1,), (1,)), ((), ())), preferred_element_type=jnp.float32
        )
        keep[s][...] += term[:split]
        send[s][...] += term[split:]


def exchange_part(occ_ints, mine, theirs, vir_ints):
    local_aux, nocc, _ = occ_ints.shape
    nvir = vir_ints.shape[1]
    states = len(mine)
    piece = pl.BlockSpec((nocc // 2, nvir), lambda p: (0, 0))
    out = jax.ShapeDtypeStruct((nocc // 2, nvir), jnp.float32)
    results = pl.pallas_call(
        functools.partial(exchange_kernel, states),
        grid=(local_aux,),
        in_specs=[pl.BlockSpec((1, nocc, nocc), lambda p: (p, 0, 0))]
        + [piece] * (2 * states)
        + [pl.BlockSpec((1, nvir, nvir), lambda p: (p, 0, 0))],
        out_specs=[piece] * (2 * states),
        out_shape=[out] * (2 * states),
        scratch_shapes=[pltpu.VMEM((nocc, states * nvir), jnp.bfloat16)],
        compiler_params=pltpu.CompilerParams(dimension_semantics=("arbitrary",)),
    )(occ_ints, *mine, *theirs, vir_ints)
    return results[:states], results[states:]


def order_columns(occ_ints, n, core):
    local_aux, nocc, _ = occ_ints.shape
    rows = nocc // n
    dest = jnp.arange(nocc)
    block, within = dest // rows, dest % rows
    upper = block // (n // 2)
    source = ((block % (n // 2)) * 2 + (upper ^ core)) * rows + within
    select = (jnp.arange(nocc)[:, None] == source[None, :]).astype(occ_ints.dtype)
    moved = jnp.dot(occ_ints.reshape(local_aux * nocc, nocc), select, preferred_element_type=jnp.float32)
    return moved.astype(occ_ints.dtype).reshape(local_aux, nocc, nocc)


def order_rows(occ_ints, n, core):
    local_aux, nocc, _ = occ_ints.shape
    o = occ_ints.reshape(local_aux, n // 2, 2, nocc // n, nocc)
    even, odd = o[:, :, 0], o[:, :, 1]
    mine = core == 0
    o = jnp.stack([jnp.where(mine, even, odd), jnp.where(mine, odd, even)], axis=1)
    return o.reshape(local_aux, nocc, nocc)


def shards(rhs, occ_energy, vir_energy, occ_ints, vir_ints):
    own_rows = rhs.shape[0]
    states = rhs.shape[1]
    nvir = rhs.shape[2]
    nocc = occ_ints.shape[1]
    n = nocc // own_rows
    assert n & (n - 1) == 0
    position = lax.axis_index("aux")
    my_occ = lax.dynamic_slice_in_dim(occ_energy, position * own_rows, own_rows, 0)
    denom = vir_energy[None, None, :] - my_occ[:, None, None]
    ordered_occ = order_columns(order_rows(occ_ints, n, position & 1), n, position & 1)
    own_denom = denom[:, 0, :]
    resps = [rhs[:, state, :] / own_denom for state in range(states)]
    for step in range(ITERS):
        got = gather_rows([resp.astype(jnp.bfloat16) for resp in resps], n, JOINT)
        keep, send = exchange_part(ordered_occ, [g[0] for g in got], [g[1] for g in got], vir_ints)
        exchange = scatter_sum(keep, send, n, JOINT)
        for state in range(states):
            resps[state] = 0.4 * resps[state] + 0.6 * (rhs[:, state, :] - exchange[state]) / own_denom
    response = jnp.stack(resps, axis=1)
    return response


def solution(mesh):
    in_specs = (
        P(("grp", "aux"), None, None),
        P("grp"),
        P("grp"),
        P(("grp", "aux"), None, None),
        P(("grp", "aux"), None, None),
    )
    out_specs = P(("grp", "aux"), None, None)
    return jax.shard_map(shards, mesh=mesh, in_specs=in_specs, out_specs=out_specs, check_vma=False)
```

```python
import functools

import jax
import jax.numpy as jnp
from jax import lax
from jax.experimental import pallas as pl
from jax.experimental.pallas import tpu as pltpu
from jax.sharding import PartitionSpec as P

ITERS = 2


def bit_orders(m, descending):
    order0 = list(range(1, m))
    order1 = list(order0)
    if len(order1) >= 2:
        order1[0], order1[1] = order1[1], order1[0]
    if descending:
        return order0[::-1] + [0], order1[::-1] + [0]
    return [0] + order0, [0] + order1


def partners(n, b0, b1):
    return [(d, d ^ (1 << (b1 if d & 1 else b0))) for d in range(n)]


def gather_rows(x, n, tie=None):
    m = n.bit_length() - 1
    me = lax.axis_index("aux")
    odd = (me & 1) == 1
    order0, order1 = bit_orders(m, True)
    acc = x[None]
    have0, have1 = [], []
    for b0, b1 in zip(order0[:-1], order1[:-1]):
        bit = jnp.where(odd, (me >> b1) & 1, (me >> b0) & 1)
        theirs = lax.ppermute(acc, "aux", partners(n, b0, b1))
        lo = jnp.where(bit == 0, acc, theirs)
        hi = jnp.where(bit == 0, theirs, acc)
        at0 = sum(1 for b in have0 if b > b0)
        at1 = sum(1 for b in have1 if b > b1)
        lead = len(have0)
        lo = lo.reshape((2,) * lead + x.shape) if lead else lo[0]
        hi = hi.reshape((2,) * lead + x.shape) if lead else hi[0]
        new0 = jnp.stack([lo, hi], axis=at0)
        if at1 == at0:
            acc = new0
        else:
            acc = jnp.where(odd, jnp.stack([lo, hi], axis=at1), new0)
        have0 = sorted(have0 + [b0], reverse=True)
        have1 = sorted(have1 + [b1], reverse=True)
        acc = acc.reshape((-1,) + x.shape)
    flat = acc.reshape((n // 2 * x.shape[0],) + x.shape[1:])
    if tie is not None:
        flat, tie = lax.optimization_barrier((flat, tie))
        return flat, lax.ppermute(flat, "aux", partners(n, 0, 0)), tie
    return flat, lax.ppermute(flat, "aux", partners(n, 0, 0))


def scatter_sum(keep, send, n):
    m = n.bit_length() - 1
    me = lax.axis_index("aux")
    odd = (me & 1) == 1
    rows = 2 * keep.shape[0] // n
    order0, order1 = bit_orders(m, False)
    shape = (2,) * (m - 1) + (rows,) + keep.shape[1:]
    acc = keep.reshape(shape) + lax.ppermute(send, "aux", partners(n, 0, 0)).reshape(shape)
    axes0 = list(range(m - 1, 0, -1))
    axes1 = list(axes0)
    for b0, b1 in zip(order0[1:], order1[1:]):
        at0, at1 = axes0.index(b0), axes1.index(b1)
        bit0, bit1 = (me >> b0) & 1, (me >> b1) & 1
        if at0 == at1:
            bit = jnp.where(odd, bit1, bit0)
            kept = lax.dynamic_index_in_dim(acc, bit, axis=at0, keepdims=False)
            sent = lax.dynamic_index_in_dim(acc, 1 - bit, axis=at0, keepdims=False)
        else:
            kept = jnp.where(
                odd,
                lax.dynamic_index_in_dim(acc, bit1, axis=at1, keepdims=False),
                lax.dynamic_index_in_dim(acc, bit0, axis=at0, keepdims=False),
            )
            sent = jnp.where(
                odd,
                lax.dynamic_index_in_dim(acc, 1 - bit1, axis=at1, keepdims=False),
                lax.dynamic_index_in_dim(acc, 1 - bit0, axis=at0, keepdims=False),
            )
        acc = kept + lax.ppermute(sent, "aux", partners(n, b0, b1))
        axes0.pop(at0)
        axes1.pop(at1)
    return acc


def exchange_kernel(states, occ_ref, *refs):
    mine, theirs = refs[:states], refs[states:2 * states]
    vir_ref = refs[2 * states]
    keep, send = refs[2 * states + 1:3 * states + 1], refs[3 * states + 1:4 * states + 1]
    r_ref = refs[4 * states + 1]
    split = mine[0].shape[0]
    nvir = vir_ref.shape[1]

    @pl.when(pl.program_id(0) == 0)
    def _():
        for s in range(states):
            keep[s][...] = jnp.zeros_like(keep[s])
            send[s][...] = jnp.zeros_like(send[s])
            r_ref[:split, s * nvir:(s + 1) * nvir] = mine[s][...]
            r_ref[split:, s * nvir:(s + 1) * nvir] = theirs[s][...]

    half = jnp.dot(occ_ref[0], r_ref[...], preferred_element_type=jnp.float32).astype(jnp.bfloat16)
    vir = vir_ref[0]
    for s in range(states):
        term = lax.dot_general(
            half[:, s * nvir:(s + 1) * nvir], vir, (((1,), (1,)), ((), ())), preferred_element_type=jnp.float32
        )
        keep[s][...] += term[:split]
        send[s][...] += term[split:]


def exchange_part(occ_ints, mine, theirs, vir_ints):
    local_aux, nocc, _ = occ_ints.shape
    nvir = vir_ints.shape[1]
    states = len(mine)
    piece = pl.BlockSpec((nocc // 2, nvir), lambda p: (0, 0))
    out = jax.ShapeDtypeStruct((nocc // 2, nvir), jnp.float32)
    results = pl.pallas_call(
        functools.partial(exchange_kernel, states),
        grid=(local_aux,),
        in_specs=[pl.BlockSpec((1, nocc, nocc), lambda p: (p, 0, 0))]
        + [piece] * (2 * states)
        + [pl.BlockSpec((1, nvir, nvir), lambda p: (p, 0, 0))],
        out_specs=[piece] * (2 * states),
        out_shape=[out] * (2 * states),
        scratch_shapes=[pltpu.VMEM((nocc, states * nvir), jnp.bfloat16)],
        compiler_params=pltpu.CompilerParams(dimension_semantics=("arbitrary",)),
    )(occ_ints, *mine, *theirs, vir_ints)
    return results[:states], results[states:]


def order_columns(occ_ints, n, core):
    local_aux, nocc, _ = occ_ints.shape
    rows = nocc // n
    dest = jnp.arange(nocc)
    block, within = dest // rows, dest % rows
    upper = block // (n // 2)
    source = ((block % (n // 2)) * 2 + (upper ^ core)) * rows + within
    select = (jnp.arange(nocc)[:, None] == source[None, :]).astype(occ_ints.dtype)
    moved = jnp.dot(occ_ints.reshape(local_aux * nocc, nocc), select, preferred_element_type=jnp.float32)
    return moved.astype(occ_ints.dtype).reshape(local_aux, nocc, nocc)


def order_rows(occ_ints, n, core):
    local_aux, nocc, _ = occ_ints.shape
    o = occ_ints.reshape(local_aux, n // 2, 2, nocc // n, nocc)
    even, odd = o[:, :, 0], o[:, :, 1]
    mine = core == 0
    o = jnp.stack([jnp.where(mine, even, odd), jnp.where(mine, odd, even)], axis=1)
    return o.reshape(local_aux, nocc, nocc)


def shards(rhs, occ_energy, vir_energy, occ_ints, vir_ints):
    own_rows = rhs.shape[0]
    states = rhs.shape[1]
    nvir = rhs.shape[2]
    nocc = occ_ints.shape[1]
    n = nocc // own_rows
    assert n & (n - 1) == 0
    position = lax.axis_index("aux")
    my_occ = lax.dynamic_slice_in_dim(occ_energy, position * own_rows, own_rows, 0)
    denom = vir_energy[None, None, :] - my_occ[:, None, None]
    ordered_occ = order_columns(order_rows(occ_ints, n, position & 1), n, position & 1)
    own_denom = denom[:, 0, :]
    resps = [rhs[:, state, :] / own_denom for state in range(states)]
    for step in range(ITERS):
        got = []
        for state, resp in enumerate(resps):
            if step == 0 and state == 0:
                mine, theirs, ordered_occ = gather_rows(resp.astype(jnp.bfloat16), n, ordered_occ)
                got.append((mine, theirs))
            else:
                got.append(gather_rows(resp.astype(jnp.bfloat16), n))
        keep, send = exchange_part(ordered_occ, [g[0] for g in got], [g[1] for g in got], vir_ints)
        for state in range(states):
            exchange = scatter_sum(keep[state], send[state], n)
            resps[state] = 0.4 * resps[state] + 0.6 * (rhs[:, state, :] - exchange) / own_denom
    response = jnp.stack(resps, axis=1)
    return response


def solution(mesh):
    in_specs = (
        P(("grp", "aux"), None, None),
        P("grp"),
        P("grp"),
        P(("grp", "aux"), None, None),
        P(("grp", "aux"), None, None),
    )
    out_specs = P(("grp", "aux"), None, None)
    return jax.shard_map(shards, mesh=mesh, in_specs=in_specs, out_specs=out_specs, check_vma=False)
```

```python
import functools

import jax
import jax.numpy as jnp
from jax import lax
from jax.experimental import pallas as pl
from jax.experimental.pallas import tpu as pltpu
from jax.sharding import PartitionSpec as P

ITERS = 2


def bit_orders(m, descending):
    order0 = list(range(1, m))
    order1 = list(order0)
    if len(order1) >= 2:
        order1[0], order1[1] = order1[1], order1[0]
    if descending:
        return order0[::-1] + [0], order1[::-1] + [0]
    return [0] + order0, [0] + order1


def partners(n, b0, b1):
    return [(d, d ^ (1 << (b1 if d & 1 else b0))) for d in range(n)]


def gather_rows(x, n):
    m = n.bit_length() - 1
    me = lax.axis_index("aux")
    odd = (me & 1) == 1
    order0, order1 = bit_orders(m, True)
    acc = x[None]
    have0, have1 = [], []
    for b0, b1 in zip(order0[:-1], order1[:-1]):
        bit = jnp.where(odd, (me >> b1) & 1, (me >> b0) & 1)
        theirs = lax.ppermute(acc, "aux", partners(n, b0, b1))
        lo = jnp.where(bit == 0, acc, theirs)
        hi = jnp.where(bit == 0, theirs, acc)
        at0 = sum(1 for b in have0 if b > b0)
        at1 = sum(1 for b in have1 if b > b1)
        lead = len(have0)
        lo = lo.reshape((2,) * lead + x.shape) if lead else lo[0]
        hi = hi.reshape((2,) * lead + x.shape) if lead else hi[0]
        new0 = jnp.stack([lo, hi], axis=at0)
        if at1 == at0:
            acc = new0
        else:
            acc = jnp.where(odd, jnp.stack([lo, hi], axis=at1), new0)
        have0 = sorted(have0 + [b0], reverse=True)
        have1 = sorted(have1 + [b1], reverse=True)
        acc = acc.reshape((-1,) + x.shape)
    flat = acc.reshape((n // 2 * x.shape[0],) + x.shape[1:])
    return flat, lax.ppermute(flat, "aux", partners(n, 0, 0))


def scatter_sum(keep, send, n):
    m = n.bit_length() - 1
    me = lax.axis_index("aux")
    odd = (me & 1) == 1
    rows = 2 * keep.shape[0] // n
    order0, order1 = bit_orders(m, False)
    shape = (2,) * (m - 1) + (rows,) + keep.shape[1:]
    acc = keep.reshape(shape) + lax.ppermute(send, "aux", partners(n, 0, 0)).reshape(shape)
    axes0 = list(range(m - 1, 0, -1))
    axes1 = list(axes0)
    for b0, b1 in zip(order0[1:], order1[1:]):
        at0, at1 = axes0.index(b0), axes1.index(b1)
        bit0, bit1 = (me >> b0) & 1, (me >> b1) & 1
        if at0 == at1:
            bit = jnp.where(odd, bit1, bit0)
            kept = lax.dynamic_index_in_dim(acc, bit, axis=at0, keepdims=False)
            sent = lax.dynamic_index_in_dim(acc, 1 - bit, axis=at0, keepdims=False)
        else:
            kept = jnp.where(
                odd,
                lax.dynamic_index_in_dim(acc, bit1, axis=at1, keepdims=False),
                lax.dynamic_index_in_dim(acc, bit0, axis=at0, keepdims=False),
            )
            sent = jnp.where(
                odd,
                lax.dynamic_index_in_dim(acc, 1 - bit1, axis=at1, keepdims=False),
                lax.dynamic_index_in_dim(acc, 1 - bit0, axis=at0, keepdims=False),
            )
        acc = kept + lax.ppermute(sent, "aux", partners(n, b0, b1))
        axes0.pop(at0)
        axes1.pop(at1)
    return acc


def exchange_kernel(states, rows, core_ref, occ_ref, *refs):
    mine, theirs = refs[:states], refs[states:2 * states]
    vir_ref = refs[2 * states]
    keep, send = refs[2 * states + 1:3 * states + 1], refs[3 * states + 1:4 * states + 1]
    r_ref = refs[4 * states + 1]
    split = mine[0].shape[0]
    nvir = vir_ref.shape[1]

    @pl.when(pl.program_id(0) == 0)
    def _():
        for s in range(states):
            cols = slice(s * nvir, (s + 1) * nvir)
            keep[s][...] = jnp.zeros_like(keep[s])
            send[s][...] = jnp.zeros_like(send[s])
            if rows:
                core = core_ref[0]
                for b in range(split // rows):
                    at_mine = pl.multiple_of((2 * b + core) * rows, rows)
                    at_theirs = pl.multiple_of((2 * b + 1 - core) * rows, rows)
                    r_ref[pl.ds(at_mine, rows), cols] = mine[s][b * rows:(b + 1) * rows]
                    r_ref[pl.ds(at_theirs, rows), cols] = theirs[s][b * rows:(b + 1) * rows]
            else:
                r_ref[:split, cols] = mine[s][...]
                r_ref[split:, cols] = theirs[s][...]

    half = jnp.dot(occ_ref[0], r_ref[...], preferred_element_type=jnp.float32).astype(jnp.bfloat16)
    vir = vir_ref[0]
    for s in range(states):
        term = lax.dot_general(
            half[:, s * nvir:(s + 1) * nvir], vir, (((1,), (1,)), ((), ())), preferred_element_type=jnp.float32
        )
        keep[s][...] += term[:split]
        send[s][...] += term[split:]


def exchange_part(core, occ_ints, mine, theirs, vir_ints, rows):
    local_aux, nocc, _ = occ_ints.shape
    nvir = vir_ints.shape[1]
    states = len(mine)
    piece = pl.BlockSpec((nocc // 2, nvir), lambda p: (0, 0))
    out = jax.ShapeDtypeStruct((nocc // 2, nvir), jnp.float32)
    results = pl.pallas_call(
        functools.partial(exchange_kernel, states, rows),
        grid=(local_aux,),
        in_specs=[pl.BlockSpec(memory_space=pltpu.SMEM), pl.BlockSpec((1, nocc, nocc), lambda p: (p, 0, 0))]
        + [piece] * (2 * states)
        + [pl.BlockSpec((1, nvir, nvir), lambda p: (p, 0, 0))],
        out_specs=[piece] * (2 * states),
        out_shape=[out] * (2 * states),
        scratch_shapes=[pltpu.VMEM((nocc, states * nvir), jnp.bfloat16)],
        compiler_params=pltpu.CompilerParams(dimension_semantics=("arbitrary",)),
    )(core, occ_ints, *mine, *theirs, vir_ints)
    return results[:states], results[states:]


def order_columns(occ_ints, n, core):
    local_aux, nocc, _ = occ_ints.shape
    rows = nocc // n
    dest = jnp.arange(nocc)
    block, within = dest // rows, dest % rows
    upper = block // (n // 2)
    source = ((block % (n // 2)) * 2 + (upper ^ core)) * rows + within
    select = (jnp.arange(nocc)[:, None] == source[None, :]).astype(occ_ints.dtype)
    moved = jnp.dot(occ_ints.reshape(local_aux * nocc, nocc), select, preferred_element_type=jnp.float32)
    return moved.astype(occ_ints.dtype).reshape(local_aux, nocc, nocc)


def order_rows(occ_ints, n, core):
    local_aux, nocc, _ = occ_ints.shape
    o = occ_ints.reshape(local_aux, n // 2, 2, nocc // n, nocc)
    even, odd = o[:, :, 0], o[:, :, 1]
    mine = core == 0
    o = jnp.stack([jnp.where(mine, even, odd), jnp.where(mine, odd, even)], axis=1)
    return o.reshape(local_aux, nocc, nocc)


def shards(rhs, occ_energy, vir_energy, occ_ints, vir_ints):
    own_rows = rhs.shape[0]
    states = rhs.shape[1]
    nvir = rhs.shape[2]
    nocc = occ_ints.shape[1]
    n = nocc // own_rows
    assert n & (n - 1) == 0
    position = lax.axis_index("aux")
    my_occ = lax.dynamic_slice_in_dim(occ_energy, position * own_rows, own_rows, 0)
    denom = vir_energy[None, None, :] - my_occ[:, None, None]
    rows = own_rows if own_rows % 16 == 0 else 0
    ordered_occ = order_rows(occ_ints, n, position & 1)
    if not rows:
        ordered_occ = order_columns(ordered_occ, n, position & 1)
    core = (position & 1).astype(jnp.int32).reshape(1)
    own_denom = denom[:, 0, :]
    resps = [rhs[:, state, :] / own_denom for state in range(states)]
    for step in range(ITERS):
        got = [gather_rows(resp.astype(jnp.bfloat16), n) for resp in resps]
        keep, send = exchange_part(core, ordered_occ, [g[0] for g in got], [g[1] for g in got], vir_ints, rows)
        for state in range(states):
            exchange = scatter_sum(keep[state], send[state], n)
            resps[state] = 0.4 * resps[state] + 0.6 * (rhs[:, state, :] - exchange) / own_denom
    response = jnp.stack(resps, axis=1)
    return response


def solution(mesh):
    in_specs = (
        P(("grp", "aux"), None, None),
        P("grp"),
        P("grp"),
        P(("grp", "aux"), None, None),
        P(("grp", "aux"), None, None),
    )
    out_specs = P(("grp", "aux"), None, None)
    return jax.shard_map(shards, mesh=mesh, in_specs=in_specs, out_specs=out_specs, check_vma=False)
```

```python
import functools

import jax
import jax.numpy as jnp
from jax import lax
from jax.experimental import pallas as pl
from jax.experimental.pallas import tpu as pltpu
from jax.sharding import PartitionSpec as P

ITERS = 2


def bit_orders(m, descending):
    order0 = list(range(1, m))
    order1 = list(order0)
    if len(order1) >= 2:
        order1[0], order1[1] = order1[1], order1[0]
    if descending:
        return order0[::-1] + [0], order1[::-1] + [0]
    return [0] + order0, [0] + order1


def partners(n, b0, b1):
    return [(d, d ^ (1 << (b1 if d & 1 else b0))) for d in range(n)]


def gather_rows(x, n):
    m = n.bit_length() - 1
    me = lax.axis_index("aux")
    odd = (me & 1) == 1
    order0, order1 = bit_orders(m, True)
    acc = x[None]
    have0, have1 = [], []
    for b0, b1 in zip(order0[:-1], order1[:-1]):
        bit = jnp.where(odd, (me >> b1) & 1, (me >> b0) & 1)
        theirs = lax.ppermute(acc, "aux", partners(n, b0, b1))
        lo = jnp.where(bit == 0, acc, theirs)
        hi = jnp.where(bit == 0, theirs, acc)
        at0 = sum(1 for b in have0 if b > b0)
        at1 = sum(1 for b in have1 if b > b1)
        lead = len(have0)
        lo = lo.reshape((2,) * lead + x.shape) if lead else lo[0]
        hi = hi.reshape((2,) * lead + x.shape) if lead else hi[0]
        new0 = jnp.stack([lo, hi], axis=at0)
        if at1 == at0:
            acc = new0
        else:
            acc = jnp.where(odd, jnp.stack([lo, hi], axis=at1), new0)
        have0 = sorted(have0 + [b0], reverse=True)
        have1 = sorted(have1 + [b1], reverse=True)
        acc = acc.reshape((-1,) + x.shape)
    flat = acc.reshape((n // 2 * x.shape[0],) + x.shape[1:])
    return flat, lax.ppermute(flat, "aux", partners(n, 0, 0))


def scatter_sum(keep, send, n):
    m = n.bit_length() - 1
    me = lax.axis_index("aux")
    odd = (me & 1) == 1
    rows = 2 * keep.shape[0] // n
    order0, order1 = bit_orders(m, False)
    shape = (2,) * (m - 1) + (rows,) + keep.shape[1:]
    acc = keep.reshape(shape) + lax.ppermute(send, "aux", partners(n, 0, 0)).reshape(shape)
    axes0 = list(range(m - 1, 0, -1))
    axes1 = list(axes0)
    for b0, b1 in zip(order0[1:], order1[1:]):
        at0, at1 = axes0.index(b0), axes1.index(b1)
        bit0, bit1 = (me >> b0) & 1, (me >> b1) & 1
        if at0 == at1:
            bit = jnp.where(odd, bit1, bit0)
            kept = lax.dynamic_index_in_dim(acc, bit, axis=at0, keepdims=False)
            sent = lax.dynamic_index_in_dim(acc, 1 - bit, axis=at0, keepdims=False)
        else:
            kept = jnp.where(
                odd,
                lax.dynamic_index_in_dim(acc, bit1, axis=at1, keepdims=False),
                lax.dynamic_index_in_dim(acc, bit0, axis=at0, keepdims=False),
            )
            sent = jnp.where(
                odd,
                lax.dynamic_index_in_dim(acc, 1 - bit1, axis=at1, keepdims=False),
                lax.dynamic_index_in_dim(acc, 1 - bit0, axis=at0, keepdims=False),
            )
        acc = kept + lax.ppermute(sent, "aux", partners(n, b0, b1))
        axes0.pop(at0)
        axes1.pop(at1)
    return acc


def exchange_kernel(states, rows, core_ref, occ_ref, *refs):
    mine, theirs = refs[:states], refs[states:2 * states]
    vir_ref = refs[2 * states]
    keep, send = refs[2 * states + 1:3 * states + 1], refs[3 * states + 1:4 * states + 1]
    r_ref, occ_buf = refs[4 * states + 1], refs[4 * states + 2]
    split = mine[0].shape[0]
    nvir = vir_ref.shape[1]

    @pl.when(pl.program_id(0) == 0)
    def _():
        if rows:
            core = core_ref[0]
            for p in range(occ_ref.shape[0]):
                for b in range(split // rows):
                    at_mine = pl.multiple_of((2 * b + core) * rows, rows)
                    at_theirs = pl.multiple_of((2 * b + 1 - core) * rows, rows)
                    occ_buf[p, b * rows:(b + 1) * rows] = occ_ref[p, pl.ds(at_mine, rows)]
                    occ_buf[p, split + b * rows:split + (b + 1) * rows] = occ_ref[p, pl.ds(at_theirs, rows)]
        for s in range(states):
            cols = slice(s * nvir, (s + 1) * nvir)
            keep[s][...] = jnp.zeros_like(keep[s])
            send[s][...] = jnp.zeros_like(send[s])
            if rows:
                core = core_ref[0]
                for b in range(split // rows):
                    at_mine = pl.multiple_of((2 * b + core) * rows, rows)
                    at_theirs = pl.multiple_of((2 * b + 1 - core) * rows, rows)
                    r_ref[pl.ds(at_mine, rows), cols] = mine[s][b * rows:(b + 1) * rows]
                    r_ref[pl.ds(at_theirs, rows), cols] = theirs[s][b * rows:(b + 1) * rows]
            else:
                r_ref[:split, cols] = mine[s][...]
                r_ref[split:, cols] = theirs[s][...]

    occ = occ_buf[pl.program_id(0)] if rows else occ_ref[pl.program_id(0)]
    half = jnp.dot(occ, r_ref[...], preferred_element_type=jnp.float32).astype(jnp.bfloat16)
    vir = vir_ref[0]
    for s in range(states):
        term = lax.dot_general(
            half[:, s * nvir:(s + 1) * nvir], vir, (((1,), (1,)), ((), ())), preferred_element_type=jnp.float32
        )
        keep[s][...] += term[:split]
        send[s][...] += term[split:]


def exchange_part(core, occ_ints, mine, theirs, vir_ints, rows):
    local_aux, nocc, _ = occ_ints.shape
    nvir = vir_ints.shape[1]
    states = len(mine)
    piece = pl.BlockSpec((nocc // 2, nvir), lambda p: (0, 0))
    out = jax.ShapeDtypeStruct((nocc // 2, nvir), jnp.float32)
    results = pl.pallas_call(
        functools.partial(exchange_kernel, states, rows),
        grid=(local_aux,),
        in_specs=[pl.BlockSpec(memory_space=pltpu.SMEM), pl.BlockSpec((local_aux, nocc, nocc), lambda p: (0, 0, 0))]
        + [piece] * (2 * states)
        + [pl.BlockSpec((1, nvir, nvir), lambda p: (p, 0, 0))],
        out_specs=[piece] * (2 * states),
        out_shape=[out] * (2 * states),
        scratch_shapes=[
            pltpu.VMEM((nocc, states * nvir), jnp.bfloat16),
            pltpu.VMEM((local_aux, nocc, nocc) if rows else (1, 8, 128), jnp.bfloat16),
        ],
        compiler_params=pltpu.CompilerParams(dimension_semantics=("arbitrary",)),
    )(core, occ_ints, *mine, *theirs, vir_ints)
    return results[:states], results[states:]


def order_columns(occ_ints, n, core):
    local_aux, nocc, _ = occ_ints.shape
    rows = nocc // n
    dest = jnp.arange(nocc)
    block, within = dest // rows, dest % rows
    upper = block // (n // 2)
    source = ((block % (n // 2)) * 2 + (upper ^ core)) * rows + within
    select = (jnp.arange(nocc)[:, None] == source[None, :]).astype(occ_ints.dtype)
    moved = jnp.dot(occ_ints.reshape(local_aux * nocc, nocc), select, preferred_element_type=jnp.float32)
    return moved.astype(occ_ints.dtype).reshape(local_aux, nocc, nocc)


def order_rows(occ_ints, n, core):
    local_aux, nocc, _ = occ_ints.shape
    o = occ_ints.reshape(local_aux, n // 2, 2, nocc // n, nocc)
    even, odd = o[:, :, 0], o[:, :, 1]
    mine = core == 0
    o = jnp.stack([jnp.where(mine, even, odd), jnp.where(mine, odd, even)], axis=1)
    return o.reshape(local_aux, nocc, nocc)


def shards(rhs, occ_energy, vir_energy, occ_ints, vir_ints):
    own_rows = rhs.shape[0]
    states = rhs.shape[1]
    nvir = rhs.shape[2]
    nocc = occ_ints.shape[1]
    n = nocc // own_rows
    assert n & (n - 1) == 0
    position = lax.axis_index("aux")
    my_occ = lax.dynamic_slice_in_dim(occ_energy, position * own_rows, own_rows, 0)
    denom = vir_energy[None, None, :] - my_occ[:, None, None]
    rows = own_rows if own_rows % 16 == 0 else 0
    ordered_occ = occ_ints
    if not rows:
        ordered_occ = order_columns(order_rows(occ_ints, n, position & 1), n, position & 1)
    core = (position & 1).astype(jnp.int32).reshape(1)
    own_denom = denom[:, 0, :]
    resps = [rhs[:, state, :] / own_denom for state in range(states)]
    for step in range(ITERS):
        got = [gather_rows(resp.astype(jnp.bfloat16), n) for resp in resps]
        keep, send = exchange_part(core, ordered_occ, [g[0] for g in got], [g[1] for g in got], vir_ints, rows)
        for state in range(states):
            exchange = scatter_sum(keep[state], send[state], n)
            resps[state] = 0.4 * resps[state] + 0.6 * (rhs[:, state, :] - exchange) / own_denom
    response = jnp.stack(resps, axis=1)
    return response


def solution(mesh):
    in_specs = (
        P(("grp", "aux"), None, None),
        P("grp"),
        P("grp"),
        P(("grp", "aux"), None, None),
        P(("grp", "aux"), None, None),
    )
    out_specs = P(("grp", "aux"), None, None)
    return jax.shard_map(shards, mesh=mesh, in_specs=in_specs, out_specs=out_specs, check_vma=False)
```

```python
import functools

import jax
import jax.numpy as jnp
from jax import lax
from jax.experimental import pallas as pl
from jax.experimental.pallas import tpu as pltpu
from jax.sharding import PartitionSpec as P

ITERS = 2


def bit_orders(m, descending):
    order0 = list(range(1, m))
    order1 = list(order0)
    if len(order1) >= 2:
        order1[0], order1[1] = order1[1], order1[0]
    if descending:
        return order0[::-1] + [0], order1[::-1] + [0]
    return [0] + order0, [0] + order1


def partners(n, b0, b1):
    return [(d, d ^ (1 << (b1 if d & 1 else b0))) for d in range(n)]


def gather_rows(x, n):
    m = n.bit_length() - 1
    me = lax.axis_index("aux")
    odd = (me & 1) == 1
    order0, order1 = bit_orders(m, True)
    acc = x[None]
    have0, have1 = [], []
    for b0, b1 in zip(order0[:-1], order1[:-1]):
        bit = jnp.where(odd, (me >> b1) & 1, (me >> b0) & 1)
        theirs = lax.ppermute(acc, "aux", partners(n, b0, b1))
        lo = jnp.where(bit == 0, acc, theirs)
        hi = jnp.where(bit == 0, theirs, acc)
        at0 = sum(1 for b in have0 if b > b0)
        at1 = sum(1 for b in have1 if b > b1)
        lead = len(have0)
        lo = lo.reshape((2,) * lead + x.shape) if lead else lo[0]
        hi = hi.reshape((2,) * lead + x.shape) if lead else hi[0]
        new0 = jnp.stack([lo, hi], axis=at0)
        if at1 == at0:
            acc = new0
        else:
            acc = jnp.where(odd, jnp.stack([lo, hi], axis=at1), new0)
        have0 = sorted(have0 + [b0], reverse=True)
        have1 = sorted(have1 + [b1], reverse=True)
        acc = acc.reshape((-1,) + x.shape)
    flat = acc.reshape((n // 2 * x.shape[0],) + x.shape[1:])
    return flat, lax.ppermute(flat, "aux", partners(n, 0, 0))


def scatter_sum(keep, send, n):
    m = n.bit_length() - 1
    me = lax.axis_index("aux")
    odd = (me & 1) == 1
    rows = 2 * keep.shape[0] // n
    order0, order1 = bit_orders(m, False)
    shape = (2,) * (m - 1) + (rows,) + keep.shape[1:]
    acc = keep.reshape(shape) + lax.ppermute(send, "aux", partners(n, 0, 0)).reshape(shape)
    axes0 = list(range(m - 1, 0, -1))
    axes1 = list(axes0)
    for b0, b1 in zip(order0[1:], order1[1:]):
        at0, at1 = axes0.index(b0), axes1.index(b1)
        bit0, bit1 = (me >> b0) & 1, (me >> b1) & 1
        if at0 == at1:
            bit = jnp.where(odd, bit1, bit0)
            kept = lax.dynamic_index_in_dim(acc, bit, axis=at0, keepdims=False)
            sent = lax.dynamic_index_in_dim(acc, 1 - bit, axis=at0, keepdims=False)
        else:
            kept = jnp.where(
                odd,
                lax.dynamic_index_in_dim(acc, bit1, axis=at1, keepdims=False),
                lax.dynamic_index_in_dim(acc, bit0, axis=at0, keepdims=False),
            )
            sent = jnp.where(
                odd,
                lax.dynamic_index_in_dim(acc, 1 - bit1, axis=at1, keepdims=False),
                lax.dynamic_index_in_dim(acc, 1 - bit0, axis=at0, keepdims=False),
            )
        acc = kept + lax.ppermute(sent, "aux", partners(n, b0, b1))
        axes0.pop(at0)
        axes1.pop(at1)
    return acc


def exchange_kernel(states, rows, core_ref, occ_ref, *refs):
    mine, theirs = refs[:states], refs[states:2 * states]
    vir_ref = refs[2 * states]
    keep, send = refs[2 * states + 1:3 * states + 1], refs[3 * states + 1:4 * states + 1]
    r_ref, occ_buf = refs[4 * states + 1], refs[4 * states + 2]
    split = mine[0].shape[0]
    nvir = vir_ref.shape[1]

    @pl.when(pl.program_id(0) == 0)
    def _():
        if rows:
            core = core_ref[0]
            for p in range(occ_ref.shape[0]):
                for b in range(split // rows):
                    at_mine = pl.multiple_of((2 * b + core) * rows, rows)
                    at_theirs = pl.multiple_of((2 * b + 1 - core) * rows, rows)
                    occ_buf[p, b * rows:(b + 1) * rows] = occ_ref[p, pl.ds(at_mine, rows)]
                    occ_buf[p, split + b * rows:split + (b + 1) * rows] = occ_ref[p, pl.ds(at_theirs, rows)]
        for s in range(states):
            cols = slice(s * nvir, (s + 1) * nvir)
            keep[s][...] = jnp.zeros_like(keep[s])
            send[s][...] = jnp.zeros_like(send[s])
            if rows:
                core = core_ref[0]
                for b in range(split // rows):
                    at_mine = pl.multiple_of((2 * b + core) * rows, rows)
                    at_theirs = pl.multiple_of((2 * b + 1 - core) * rows, rows)
                    r_ref[pl.ds(at_mine, rows), cols] = mine[s][b * rows:(b + 1) * rows]
                    r_ref[pl.ds(at_theirs, rows), cols] = theirs[s][b * rows:(b + 1) * rows]
            else:
                r_ref[:split, cols] = mine[s][...]
                r_ref[split:, cols] = theirs[s][...]

    occ = occ_buf[pl.program_id(0)] if rows else occ_ref[pl.program_id(0)]
    half = jnp.dot(occ, r_ref[...], preferred_element_type=jnp.float32).astype(jnp.bfloat16)
    vir = vir_ref[0]
    for s in range(states):
        term = lax.dot_general(
            half[:, s * nvir:(s + 1) * nvir], vir, (((1,), (1,)), ((), ())), preferred_element_type=jnp.float32
        )
        keep[s][...] += term[:split]
        send[s][...] += term[split:]


def exchange_part(core, occ_ints, mine, theirs, vir_ints, rows):
    local_aux, nocc, _ = occ_ints.shape
    nvir = vir_ints.shape[1]
    states = len(mine)
    piece = pl.BlockSpec((nocc // 2, nvir), lambda p: (0, 0))
    out = jax.ShapeDtypeStruct((nocc // 2, nvir), jnp.float32)
    results = pl.pallas_call(
        functools.partial(exchange_kernel, states, rows),
        grid=(local_aux,),
        in_specs=[pl.BlockSpec(memory_space=pltpu.SMEM), pl.BlockSpec((local_aux, nocc, nocc), lambda p: (0, 0, 0))]
        + [piece] * (2 * states)
        + [pl.BlockSpec((1, nvir, nvir), lambda p: (p, 0, 0))],
        out_specs=[piece] * (2 * states),
        out_shape=[out] * (2 * states),
        scratch_shapes=[
            pltpu.VMEM((nocc, states * nvir), jnp.bfloat16),
            pltpu.VMEM((local_aux, nocc, nocc) if rows else (1, 8, 128), jnp.bfloat16),
        ],
        compiler_params=pltpu.CompilerParams(dimension_semantics=("arbitrary",)),
    )(core, occ_ints, *mine, *theirs, vir_ints)
    return results[:states], results[states:]


def order_columns(occ_ints, n, core):
    local_aux, nocc, _ = occ_ints.shape
    rows = nocc // n
    dest = jnp.arange(nocc)
    block, within = dest // rows, dest % rows
    upper = block // (n // 2)
    source = ((block % (n // 2)) * 2 + (upper ^ core)) * rows + within
    select = (jnp.arange(nocc)[:, None] == source[None, :]).astype(occ_ints.dtype)
    moved = jnp.dot(occ_ints.reshape(local_aux * nocc, nocc), select, preferred_element_type=jnp.float32)
    return moved.astype(occ_ints.dtype).reshape(local_aux, nocc, nocc)


def order_rows(occ_ints, n, core):
    local_aux, nocc, _ = occ_ints.shape
    o = occ_ints.reshape(local_aux, n // 2, 2, nocc // n, nocc)
    even, odd = o[:, :, 0], o[:, :, 1]
    mine = core == 0
    o = jnp.stack([jnp.where(mine, even, odd), jnp.where(mine, odd, even)], axis=1)
    return o.reshape(local_aux, nocc, nocc)


def shards(rhs, occ_energy, vir_energy, occ_ints, vir_ints):
    own_rows = rhs.shape[0]
    states = rhs.shape[1]
    nvir = rhs.shape[2]
    nocc = occ_ints.shape[1]
    n = nocc // own_rows
    assert n & (n - 1) == 0
    position = lax.axis_index("aux")
    wanted = position * own_rows + jnp.arange(own_rows)
    my_occ = jnp.sum(jnp.where(jnp.arange(nocc)[None, :] == wanted[:, None], occ_energy[None, :], 0.0), axis=1)
    denom = vir_energy[None, None, :] - my_occ[:, None, None]
    rows = own_rows if own_rows % 16 == 0 else 0
    ordered_occ = occ_ints
    if not rows:
        ordered_occ = order_columns(order_rows(occ_ints, n, position & 1), n, position & 1)
    core = (position & 1).astype(jnp.int32).reshape(1)
    own_denom = denom[:, 0, :]
    resps = [rhs[:, state, :] / own_denom for state in range(states)]
    for step in range(ITERS):
        got = [gather_rows(resp.astype(jnp.bfloat16), n) for resp in resps]
        keep, send = exchange_part(core, ordered_occ, [g[0] for g in got], [g[1] for g in got], vir_ints, rows)
        for state in range(states):
            exchange = scatter_sum(keep[state], send[state], n)
            resps[state] = 0.4 * resps[state] + 0.6 * (rhs[:, state, :] - exchange) / own_denom
    response = jnp.stack(resps, axis=1)
    return response


def solution(mesh):
    in_specs = (
        P(("grp", "aux"), None, None),
        P("grp"),
        P("grp"),
        P(("grp", "aux"), None, None),
        P(("grp", "aux"), None, None),
    )
    out_specs = P(("grp", "aux"), None, None)
    return jax.shard_map(shards, mesh=mesh, in_specs=in_specs, out_specs=out_specs, check_vma=False)
```

```python
import functools

import jax
import jax.numpy as jnp
from jax import lax
from jax.experimental import pallas as pl
from jax.experimental.pallas import tpu as pltpu
from jax.sharding import PartitionSpec as P

ITERS = 2


def bit_orders(m, descending):
    order0 = list(range(1, m))
    order1 = list(order0)
    if len(order1) >= 2:
        order1[0], order1[1] = order1[1], order1[0]
    if descending:
        return order0[::-1] + [0], order1[::-1] + [0]
    return [0] + order0, [0] + order1


def partners(n, b0, b1):
    return [(d, d ^ (1 << (b1 if d & 1 else b0))) for d in range(n)]


def gather_rows(x, n):
    m = n.bit_length() - 1
    me = lax.axis_index("aux")
    odd = (me & 1) == 1
    order0, order1 = bit_orders(m, True)
    acc = x[None]
    have0, have1 = [], []
    for b0, b1 in zip(order0[:-1], order1[:-1]):
        bit = jnp.where(odd, (me >> b1) & 1, (me >> b0) & 1)
        theirs = lax.ppermute(acc, "aux", partners(n, b0, b1))
        lo = jnp.where(bit == 0, acc, theirs)
        hi = jnp.where(bit == 0, theirs, acc)
        at0 = sum(1 for b in have0 if b > b0)
        at1 = sum(1 for b in have1 if b > b1)
        lead = len(have0)
        lo = lo.reshape((2,) * lead + x.shape) if lead else lo[0]
        hi = hi.reshape((2,) * lead + x.shape) if lead else hi[0]
        new0 = jnp.stack([lo, hi], axis=at0)
        if at1 == at0:
            acc = new0
        else:
            acc = jnp.where(odd, jnp.stack([lo, hi], axis=at1), new0)
        have0 = sorted(have0 + [b0], reverse=True)
        have1 = sorted(have1 + [b1], reverse=True)
        acc = acc.reshape((-1,) + x.shape)
    flat = acc.reshape((n // 2 * x.shape[0],) + x.shape[1:])
    return flat, lax.ppermute(flat, "aux", partners(n, 0, 0))


def scatter_sum(keep, send, n):
    m = n.bit_length() - 1
    me = lax.axis_index("aux")
    odd = (me & 1) == 1
    rows = 2 * keep.shape[0] // n
    order0, order1 = bit_orders(m, False)
    shape = (2,) * (m - 1) + (rows,) + keep.shape[1:]
    acc = keep.reshape(shape) + lax.ppermute(send, "aux", partners(n, 0, 0)).reshape(shape)
    axes0 = list(range(m - 1, 0, -1))
    axes1 = list(axes0)
    for b0, b1 in zip(order0[1:], order1[1:]):
        at0, at1 = axes0.index(b0), axes1.index(b1)
        bit0, bit1 = (me >> b0) & 1, (me >> b1) & 1
        if at0 == at1:
            bit = jnp.where(odd, bit1, bit0)
            kept = lax.dynamic_index_in_dim(acc, bit, axis=at0, keepdims=False)
            sent = lax.dynamic_index_in_dim(acc, 1 - bit, axis=at0, keepdims=False)
        else:
            kept = jnp.where(
                odd,
                lax.dynamic_index_in_dim(acc, bit1, axis=at1, keepdims=False),
                lax.dynamic_index_in_dim(acc, bit0, axis=at0, keepdims=False),
            )
            sent = jnp.where(
                odd,
                lax.dynamic_index_in_dim(acc, 1 - bit1, axis=at1, keepdims=False),
                lax.dynamic_index_in_dim(acc, 1 - bit0, axis=at0, keepdims=False),
            )
        acc = kept + lax.ppermute(sent, "aux", partners(n, b0, b1))
        axes0.pop(at0)
        axes1.pop(at1)
    return acc


def exchange_kernel(states, rows, core_ref, occ_ref, *refs):
    mine, theirs = refs[:states], refs[states:2 * states]
    vir_ref = refs[2 * states]
    keep, send = refs[2 * states + 1:3 * states + 1], refs[3 * states + 1:4 * states + 1]
    r_ref, occ_buf = refs[4 * states + 1], refs[4 * states + 2]
    split = mine[0].shape[0]
    nvir = vir_ref.shape[1]

    @pl.when(pl.program_id(0) == 0)
    def _():
        if rows:
            core = core_ref[0]
            for p in range(occ_ref.shape[0]):
                for b in range(split // rows):
                    at_mine = pl.multiple_of((2 * b + core) * rows, rows)
                    at_theirs = pl.multiple_of((2 * b + 1 - core) * rows, rows)
                    occ_buf[p, b * rows:(b + 1) * rows] = occ_ref[p, pl.ds(at_mine, rows)]
                    occ_buf[p, split + b * rows:split + (b + 1) * rows] = occ_ref[p, pl.ds(at_theirs, rows)]
        for s in range(states):
            cols = slice(s * nvir, (s + 1) * nvir)
            keep[s][...] = jnp.zeros_like(keep[s])
            send[s][...] = jnp.zeros_like(send[s])
            if rows:
                core = core_ref[0]
                for b in range(split // rows):
                    at_mine = pl.multiple_of((2 * b + core) * rows, rows)
                    at_theirs = pl.multiple_of((2 * b + 1 - core) * rows, rows)
                    r_ref[pl.ds(at_mine, rows), cols] = mine[s][b * rows:(b + 1) * rows]
                    r_ref[pl.ds(at_theirs, rows), cols] = theirs[s][b * rows:(b + 1) * rows]
            else:
                r_ref[:split, cols] = mine[s][...]
                r_ref[split:, cols] = theirs[s][...]

    occ = occ_buf[pl.program_id(0)] if rows else occ_ref[pl.program_id(0)]
    half = jnp.dot(occ, r_ref[...], preferred_element_type=jnp.float32).astype(jnp.bfloat16)
    vir = vir_ref[0]
    for s in range(states):
        term = lax.dot_general(
            half[:, s * nvir:(s + 1) * nvir], vir, (((1,), (1,)), ((), ())), preferred_element_type=jnp.float32
        )
        keep[s][...] += term[:split]
        send[s][...] += term[split:]


def exchange_part(core, occ_ints, mine, theirs, vir_ints, rows):
    local_aux, nocc, _ = occ_ints.shape
    nvir = vir_ints.shape[1]
    states = len(mine)
    piece = pl.BlockSpec((nocc // 2, nvir), lambda p: (0, 0))
    out = jax.ShapeDtypeStruct((nocc // 2, nvir), jnp.float32)
    results = pl.pallas_call(
        functools.partial(exchange_kernel, states, rows),
        grid=(local_aux,),
        in_specs=[pl.BlockSpec(memory_space=pltpu.SMEM), pl.BlockSpec((local_aux, nocc, nocc), lambda p: (0, 0, 0))]
        + [piece] * (2 * states)
        + [pl.BlockSpec((1, nvir, nvir), lambda p: (p, 0, 0))],
        out_specs=[piece] * (2 * states),
        out_shape=[out] * (2 * states),
        scratch_shapes=[
            pltpu.VMEM((nocc, states * nvir), jnp.bfloat16),
            pltpu.VMEM((local_aux, nocc, nocc) if rows else (1, 8, 128), jnp.bfloat16),
        ],
        compiler_params=pltpu.CompilerParams(dimension_semantics=("arbitrary",)),
    )(core, occ_ints, *mine, *theirs, vir_ints)
    return results[:states], results[states:]


def order_columns(occ_ints, n, core):
    local_aux, nocc, _ = occ_ints.shape
    rows = nocc // n
    dest = jnp.arange(nocc)
    block, within = dest // rows, dest % rows
    upper = block // (n // 2)
    source = ((block % (n // 2)) * 2 + (upper ^ core)) * rows + within
    select = (jnp.arange(nocc)[:, None] == source[None, :]).astype(occ_ints.dtype)
    moved = jnp.dot(occ_ints.reshape(local_aux * nocc, nocc), select, preferred_element_type=jnp.float32)
    return moved.astype(occ_ints.dtype).reshape(local_aux, nocc, nocc)


def order_rows(occ_ints, n, core):
    local_aux, nocc, _ = occ_ints.shape
    o = occ_ints.reshape(local_aux, n // 2, 2, nocc // n, nocc)
    even, odd = o[:, :, 0], o[:, :, 1]
    mine = core == 0
    o = jnp.stack([jnp.where(mine, even, odd), jnp.where(mine, odd, even)], axis=1)
    return o.reshape(local_aux, nocc, nocc)


def shards(rhs, occ_energy, vir_energy, occ_ints, vir_ints):
    own_rows = rhs.shape[0]
    states = rhs.shape[1]
    nvir = rhs.shape[2]
    nocc = occ_ints.shape[1]
    n = nocc // own_rows
    assert n & (n - 1) == 0
    position = lax.axis_index("aux")
    wanted = position * own_rows + jnp.arange(own_rows)
    my_occ = jnp.sum(jnp.where(jnp.arange(nocc)[None, :] == wanted[:, None], occ_energy[None, :], 0.0), axis=1)
    denom = vir_energy[None, None, :] - my_occ[:, None, None]
    rows = own_rows if own_rows % 16 == 0 else 0
    ordered_occ = occ_ints
    if not rows:
        ordered_occ = order_columns(order_rows(occ_ints, n, position & 1), n, position & 1)
    core = (position & 1).astype(jnp.int32).reshape(1)
    own_denom = denom[:, 0, :]
    resps = [rhs[:, state, :] / own_denom for state in range(states)]
    first = (rhs / denom).astype(jnp.bfloat16)
    for step in range(ITERS):
        rounded = [first[:, state, :] for state in range(states)] if step == 0 else [
            resp.astype(jnp.bfloat16) for resp in resps
        ]
        got = [gather_rows(r, n) for r in rounded]
        keep, send = exchange_part(core, ordered_occ, [g[0] for g in got], [g[1] for g in got], vir_ints, rows)
        for state in range(states):
            exchange = scatter_sum(keep[state], send[state], n)
            resps[state] = 0.4 * resps[state] + 0.6 * (rhs[:, state, :] - exchange) / own_denom
    response = jnp.stack(resps, axis=1)
    return response


def solution(mesh):
    in_specs = (
        P(("grp", "aux"), None, None),
        P("grp"),
        P("grp"),
        P(("grp", "aux"), None, None),
        P(("grp", "aux"), None, None),
    )
    out_specs = P(("grp", "aux"), None, None)
    return jax.shard_map(shards, mesh=mesh, in_specs=in_specs, out_specs=out_specs, check_vma=False)
```

```python
import functools

import jax
import jax.numpy as jnp
from jax import lax
from jax.experimental import pallas as pl
from jax.experimental.pallas import tpu as pltpu
from jax.sharding import PartitionSpec as P

ITERS = 2


def bit_orders(m, descending):
    order0 = list(range(1, m))
    order1 = list(order0)
    if len(order1) >= 2:
        order1[0], order1[1] = order1[1], order1[0]
    if descending:
        return order0[::-1] + [0], order1[::-1] + [0]
    return [0] + order0, [0] + order1


def partners(n, b0, b1):
    return [(d, d ^ (1 << (b1 if d & 1 else b0))) for d in range(n)]


def gather_rows(x, n):
    m = n.bit_length() - 1
    me = lax.axis_index("aux")
    odd = (me & 1) == 1
    order0, order1 = bit_orders(m, True)
    acc = x[None]
    have0, have1 = [], []
    for b0, b1 in zip(order0[:-1], order1[:-1]):
        bit = jnp.where(odd, (me >> b1) & 1, (me >> b0) & 1)
        theirs = lax.ppermute(acc, "aux", partners(n, b0, b1))
        lo = jnp.where(bit == 0, acc, theirs)
        hi = jnp.where(bit == 0, theirs, acc)
        at0 = sum(1 for b in have0 if b > b0)
        at1 = sum(1 for b in have1 if b > b1)
        lead = len(have0)
        lo = lo.reshape((2,) * lead + x.shape) if lead else lo[0]
        hi = hi.reshape((2,) * lead + x.shape) if lead else hi[0]
        new0 = jnp.stack([lo, hi], axis=at0)
        if at1 == at0:
            acc = new0
        else:
            acc = jnp.where(odd, jnp.stack([lo, hi], axis=at1), new0)
        have0 = sorted(have0 + [b0], reverse=True)
        have1 = sorted(have1 + [b1], reverse=True)
        acc = acc.reshape((-1,) + x.shape)
    flat = acc.reshape((n // 2 * x.shape[0],) + x.shape[1:])
    return flat, lax.ppermute(flat, "aux", partners(n, 0, 0))


def scatter_sum(keep, send, n):
    m = n.bit_length() - 1
    me = lax.axis_index("aux")
    odd = (me & 1) == 1
    rows = 2 * keep.shape[0] // n
    order0, order1 = bit_orders(m, False)
    shape = (2,) * (m - 1) + (rows,) + keep.shape[1:]
    acc = keep.reshape(shape) + lax.ppermute(send, "aux", partners(n, 0, 0)).reshape(shape)
    axes0 = list(range(m - 1, 0, -1))
    axes1 = list(axes0)
    for b0, b1 in zip(order0[1:], order1[1:]):
        at0, at1 = axes0.index(b0), axes1.index(b1)
        bit0, bit1 = (me >> b0) & 1, (me >> b1) & 1
        if at0 == at1:
            bit = jnp.where(odd, bit1, bit0)
            kept = lax.dynamic_index_in_dim(acc, bit, axis=at0, keepdims=False)
            sent = lax.dynamic_index_in_dim(acc, 1 - bit, axis=at0, keepdims=False)
        else:
            kept = jnp.where(
                odd,
                lax.dynamic_index_in_dim(acc, bit1, axis=at1, keepdims=False),
                lax.dynamic_index_in_dim(acc, bit0, axis=at0, keepdims=False),
            )
            sent = jnp.where(
                odd,
                lax.dynamic_index_in_dim(acc, 1 - bit1, axis=at1, keepdims=False),
                lax.dynamic_index_in_dim(acc, 1 - bit0, axis=at0, keepdims=False),
            )
        acc = kept + lax.ppermute(sent, "aux", partners(n, b0, b1))
        axes0.pop(at0)
        axes1.pop(at1)
    return acc


def exchange_kernel(states, rows, core_ref, occ_ref, *refs):
    mine, theirs = refs[:states], refs[states:2 * states]
    vir_ref = refs[2 * states]
    keep, send = refs[2 * states + 1:3 * states + 1], refs[3 * states + 1:4 * states + 1]
    r_ref, occ_buf = refs[4 * states + 1], refs[4 * states + 2]
    split = mine[0].shape[0]
    nvir = vir_ref.shape[1]

    @pl.when(pl.program_id(0) == 0)
    def _():
        if rows:
            core = core_ref[0]
            for p in range(occ_ref.shape[0]):
                for b in range(split // rows):
                    at_mine = pl.multiple_of((2 * b + core) * rows, rows)
                    at_theirs = pl.multiple_of((2 * b + 1 - core) * rows, rows)
                    occ_buf[p, b * rows:(b + 1) * rows] = occ_ref[p, pl.ds(at_mine, rows)]
                    occ_buf[p, split + b * rows:split + (b + 1) * rows] = occ_ref[p, pl.ds(at_theirs, rows)]
        for s in range(states):
            cols = slice(s * nvir, (s + 1) * nvir)
            keep[s][...] = jnp.zeros_like(keep[s])
            send[s][...] = jnp.zeros_like(send[s])
            if rows:
                core = core_ref[0]
                for b in range(split // rows):
                    at_mine = pl.multiple_of((2 * b + core) * rows, rows)
                    at_theirs = pl.multiple_of((2 * b + 1 - core) * rows, rows)
                    r_ref[pl.ds(at_mine, rows), cols] = mine[s][b * rows:(b + 1) * rows]
                    r_ref[pl.ds(at_theirs, rows), cols] = theirs[s][b * rows:(b + 1) * rows]
            else:
                r_ref[:split, cols] = mine[s][...]
                r_ref[split:, cols] = theirs[s][...]

    occ = occ_buf[pl.program_id(0)] if rows else occ_ref[pl.program_id(0)]
    half = jnp.dot(occ, r_ref[...], preferred_element_type=jnp.float32).astype(jnp.bfloat16)
    vir = vir_ref[0]
    for s in range(states):
        term = lax.dot_general(
            half[:, s * nvir:(s + 1) * nvir], vir, (((1,), (1,)), ((), ())), preferred_element_type=jnp.float32
        )
        keep[s][...] += term[:split]
        send[s][...] += term[split:]


def exchange_part(core, occ_ints, mine, theirs, vir_ints, rows):
    local_aux, nocc, _ = occ_ints.shape
    nvir = vir_ints.shape[1]
    states = len(mine)
    piece = pl.BlockSpec((nocc // 2, nvir), lambda p: (0, 0))
    out = jax.ShapeDtypeStruct((nocc // 2, nvir), jnp.float32)
    results = pl.pallas_call(
        functools.partial(exchange_kernel, states, rows),
        grid=(local_aux,),
        in_specs=[pl.BlockSpec(memory_space=pltpu.SMEM), pl.BlockSpec((local_aux, nocc, nocc), lambda p: (0, 0, 0))]
        + [piece] * (2 * states)
        + [pl.BlockSpec((1, nvir, nvir), lambda p: (p, 0, 0))],
        out_specs=[piece] * (2 * states),
        out_shape=[out] * (2 * states),
        scratch_shapes=[
            pltpu.VMEM((nocc, states * nvir), jnp.bfloat16),
            pltpu.VMEM((local_aux, nocc, nocc) if rows else (1, 8, 128), jnp.bfloat16),
        ],
        compiler_params=pltpu.CompilerParams(dimension_semantics=("arbitrary",)),
    )(core, occ_ints, *mine, *theirs, vir_ints)
    return results[:states], results[states:]


def order_columns(occ_ints, n, core):
    local_aux, nocc, _ = occ_ints.shape
    rows = nocc // n
    dest = jnp.arange(nocc)
    block, within = dest // rows, dest % rows
    upper = block // (n // 2)
    source = ((block % (n // 2)) * 2 + (upper ^ core)) * rows + within
    select = (jnp.arange(nocc)[:, None] == source[None, :]).astype(occ_ints.dtype)
    moved = jnp.dot(occ_ints.reshape(local_aux * nocc, nocc), select, preferred_element_type=jnp.float32)
    return moved.astype(occ_ints.dtype).reshape(local_aux, nocc, nocc)


def order_rows(occ_ints, n, core):
    local_aux, nocc, _ = occ_ints.shape
    o = occ_ints.reshape(local_aux, n // 2, 2, nocc // n, nocc)
    even, odd = o[:, :, 0], o[:, :, 1]
    mine = core == 0
    o = jnp.stack([jnp.where(mine, even, odd), jnp.where(mine, odd, even)], axis=1)
    return o.reshape(local_aux, nocc, nocc)


def shards(rhs, occ_energy, vir_energy, occ_ints, vir_ints):
    own_rows = rhs.shape[0]
    states = rhs.shape[1]
    nvir = rhs.shape[2]
    nocc = occ_ints.shape[1]
    n = nocc // own_rows
    assert n & (n - 1) == 0
    position = lax.axis_index("aux")
    wanted = position * own_rows + jnp.arange(own_rows)
    my_occ = jnp.sum(jnp.where(jnp.arange(nocc)[None, :] == wanted[:, None], occ_energy[None, :], 0.0), axis=1)
    denom = vir_energy[None, None, :] - my_occ[:, None, None]
    rows = own_rows if own_rows % 16 == 0 else 0
    ordered_occ = occ_ints
    if not rows:
        ordered_occ = order_columns(order_rows(occ_ints, n, position & 1), n, position & 1)
    core = (position & 1).astype(jnp.int32).reshape(1)
    own_denom = denom[:, 0, :]
    resps = [rhs[:, state, :] / own_denom for state in range(states)]
    for step in range(ITERS):
        got = [gather_rows(resp.astype(jnp.bfloat16), n) for resp in resps]
        if step < ITERS - 1:
            calls = [exchange_part(core, ordered_occ, [g[0]], [g[1]], vir_ints, rows) for g in got]
            keep, send = [c[0][0] for c in calls], [c[1][0] for c in calls]
        else:
            keep, send = exchange_part(core, ordered_occ, [g[0] for g in got], [g[1] for g in got], vir_ints, rows)
        for state in range(states):
            exchange = scatter_sum(keep[state], send[state], n)
            resps[state] = 0.4 * resps[state] + 0.6 * (rhs[:, state, :] - exchange) / own_denom
    response = jnp.stack(resps, axis=1)
    return response


def solution(mesh):
    in_specs = (
        P(("grp", "aux"), None, None),
        P("grp"),
        P("grp"),
        P(("grp", "aux"), None, None),
        P(("grp", "aux"), None, None),
    )
    out_specs = P(("grp", "aux"), None, None)
    return jax.shard_map(shards, mesh=mesh, in_specs=in_specs, out_specs=out_specs, check_vma=False)
```

```python
import functools

import jax
import jax.numpy as jnp
from jax import lax
from jax.experimental import pallas as pl
from jax.experimental.pallas import tpu as pltpu
from jax.sharding import PartitionSpec as P

ITERS = 2


def bit_orders(m, descending):
    order0 = list(range(1, m))
    order1 = list(order0)
    if len(order1) >= 2:
        order1[0], order1[1] = order1[1], order1[0]
    if descending:
        return order0[::-1] + [0], order1[::-1] + [0]
    return [0] + order0, [0] + order1


def partners(n, b0, b1):
    return [(d, d ^ (1 << (b1 if d & 1 else b0))) for d in range(n)]


def gather_rows(x, n):
    m = n.bit_length() - 1
    me = lax.axis_index("aux")
    odd = (me & 1) == 1
    order0, order1 = bit_orders(m, True)
    acc = x[None]
    have0, have1 = [], []
    for b0, b1 in zip(order0[:-1], order1[:-1]):
        bit = jnp.where(odd, (me >> b1) & 1, (me >> b0) & 1)
        theirs = lax.ppermute(acc, "aux", partners(n, b0, b1))
        lo = jnp.where(bit == 0, acc, theirs)
        hi = jnp.where(bit == 0, theirs, acc)
        at0 = sum(1 for b in have0 if b > b0)
        at1 = sum(1 for b in have1 if b > b1)
        lead = len(have0)
        lo = lo.reshape((2,) * lead + x.shape) if lead else lo[0]
        hi = hi.reshape((2,) * lead + x.shape) if lead else hi[0]
        new0 = jnp.stack([lo, hi], axis=at0)
        if at1 == at0:
            acc = new0
        else:
            acc = jnp.where(odd, jnp.stack([lo, hi], axis=at1), new0)
        have0 = sorted(have0 + [b0], reverse=True)
        have1 = sorted(have1 + [b1], reverse=True)
        acc = acc.reshape((-1,) + x.shape)
    flat = acc.reshape((n // 2 * x.shape[0],) + x.shape[1:])
    return flat, lax.ppermute(flat, "aux", partners(n, 0, 0))


def scatter_sum(keep, send, n):
    m = n.bit_length() - 1
    me = lax.axis_index("aux")
    odd = (me & 1) == 1
    rows = 2 * keep.shape[0] // n
    order0, order1 = bit_orders(m, False)
    shape = (2,) * (m - 1) + (rows,) + keep.shape[1:]
    acc = keep.reshape(shape) + lax.ppermute(send, "aux", partners(n, 0, 0)).reshape(shape)
    axes0 = list(range(m - 1, 0, -1))
    axes1 = list(axes0)
    for b0, b1 in zip(order0[1:], order1[1:]):
        at0, at1 = axes0.index(b0), axes1.index(b1)
        bit0, bit1 = (me >> b0) & 1, (me >> b1) & 1
        if at0 == at1:
            bit = jnp.where(odd, bit1, bit0)
            kept = lax.dynamic_index_in_dim(acc, bit, axis=at0, keepdims=False)
            sent = lax.dynamic_index_in_dim(acc, 1 - bit, axis=at0, keepdims=False)
        else:
            kept = jnp.where(
                odd,
                lax.dynamic_index_in_dim(acc, bit1, axis=at1, keepdims=False),
                lax.dynamic_index_in_dim(acc, bit0, axis=at0, keepdims=False),
            )
            sent = jnp.where(
                odd,
                lax.dynamic_index_in_dim(acc, 1 - bit1, axis=at1, keepdims=False),
                lax.dynamic_index_in_dim(acc, 1 - bit0, axis=at0, keepdims=False),
            )
        acc = kept + lax.ppermute(sent, "aux", partners(n, b0, b1))
        axes0.pop(at0)
        axes1.pop(at1)
    return acc


def exchange_kernel(states, rows, core_ref, occ_ref, *refs):
    mine, theirs = refs[:states], refs[states:2 * states]
    vir_ref = refs[2 * states]
    keep, send = refs[2 * states + 1:3 * states + 1], refs[3 * states + 1:4 * states + 1]
    r_ref, occ_buf = refs[4 * states + 1], refs[4 * states + 2]
    split = mine[0].shape[0]
    nvir = vir_ref.shape[1]

    @pl.when(pl.program_id(0) == 0)
    def _():
        if rows:
            core = core_ref[0]
            for p in range(occ_ref.shape[0]):
                for b in range(split // rows):
                    at_mine = pl.multiple_of((2 * b + core) * rows, rows)
                    at_theirs = pl.multiple_of((2 * b + 1 - core) * rows, rows)
                    occ_buf[p, b * rows:(b + 1) * rows] = occ_ref[p, pl.ds(at_mine, rows)]
                    occ_buf[p, split + b * rows:split + (b + 1) * rows] = occ_ref[p, pl.ds(at_theirs, rows)]
        for s in range(states):
            cols = slice(s * nvir, (s + 1) * nvir)
            if rows:
                core = core_ref[0]
                for b in range(split // rows):
                    at_mine = pl.multiple_of((2 * b + core) * rows, rows)
                    at_theirs = pl.multiple_of((2 * b + 1 - core) * rows, rows)
                    r_ref[pl.ds(at_mine, rows), cols] = mine[s][b * rows:(b + 1) * rows]
                    r_ref[pl.ds(at_theirs, rows), cols] = theirs[s][b * rows:(b + 1) * rows]
            else:
                r_ref[:split, cols] = mine[s][...]
                r_ref[split:, cols] = theirs[s][...]

    occ = occ_buf[pl.program_id(0)] if rows else occ_ref[pl.program_id(0)]
    half = jnp.dot(occ, r_ref[...], preferred_element_type=jnp.float32).astype(jnp.bfloat16)
    vir = vir_ref[0]
    for s in range(states):
        term = lax.dot_general(
            half[:, s * nvir:(s + 1) * nvir], vir, (((1,), (1,)), ((), ())), preferred_element_type=jnp.float32
        )

        @pl.when(pl.program_id(0) == 0)
        def _():
            keep[s][...] = term[:split]
            send[s][...] = term[split:]

        @pl.when(pl.program_id(0) > 0)
        def _():
            keep[s][...] += term[:split]
            send[s][...] += term[split:]


def exchange_part(core, occ_ints, mine, theirs, vir_ints, rows):
    local_aux, nocc, _ = occ_ints.shape
    nvir = vir_ints.shape[1]
    states = len(mine)
    piece = pl.BlockSpec((nocc // 2, nvir), lambda p: (0, 0))
    out = jax.ShapeDtypeStruct((nocc // 2, nvir), jnp.float32)
    results = pl.pallas_call(
        functools.partial(exchange_kernel, states, rows),
        grid=(local_aux,),
        in_specs=[pl.BlockSpec(memory_space=pltpu.SMEM), pl.BlockSpec((local_aux, nocc, nocc), lambda p: (0, 0, 0))]
        + [piece] * (2 * states)
        + [pl.BlockSpec((1, nvir, nvir), lambda p: (p, 0, 0))],
        out_specs=[piece] * (2 * states),
        out_shape=[out] * (2 * states),
        scratch_shapes=[
            pltpu.VMEM((nocc, states * nvir), jnp.bfloat16),
            pltpu.VMEM((local_aux, nocc, nocc) if rows else (1, 8, 128), jnp.bfloat16),
        ],
        compiler_params=pltpu.CompilerParams(dimension_semantics=("arbitrary",)),
    )(core, occ_ints, *mine, *theirs, vir_ints)
    return results[:states], results[states:]


def order_columns(occ_ints, n, core):
    local_aux, nocc, _ = occ_ints.shape
    rows = nocc // n
    dest = jnp.arange(nocc)
    block, within = dest // rows, dest % rows
    upper = block // (n // 2)
    source = ((block % (n // 2)) * 2 + (upper ^ core)) * rows + within
    select = (jnp.arange(nocc)[:, None] == source[None, :]).astype(occ_ints.dtype)
    moved = jnp.dot(occ_ints.reshape(local_aux * nocc, nocc), select, preferred_element_type=jnp.float32)
    return moved.astype(occ_ints.dtype).reshape(local_aux, nocc, nocc)


def order_rows(occ_ints, n, core):
    local_aux, nocc, _ = occ_ints.shape
    o = occ_ints.reshape(local_aux, n // 2, 2, nocc // n, nocc)
    even, odd = o[:, :, 0], o[:, :, 1]
    mine = core == 0
    o = jnp.stack([jnp.where(mine, even, odd), jnp.where(mine, odd, even)], axis=1)
    return o.reshape(local_aux, nocc, nocc)


def shards(rhs, occ_energy, vir_energy, occ_ints, vir_ints):
    own_rows = rhs.shape[0]
    states = rhs.shape[1]
    nvir = rhs.shape[2]
    nocc = occ_ints.shape[1]
    n = nocc // own_rows
    assert n & (n - 1) == 0
    position = lax.axis_index("aux")
    wanted = position * own_rows + jnp.arange(own_rows)
    my_occ = jnp.sum(jnp.where(jnp.arange(nocc)[None, :] == wanted[:, None], occ_energy[None, :], 0.0), axis=1)
    denom = vir_energy[None, None, :] - my_occ[:, None, None]
    rows = own_rows if own_rows % 16 == 0 else 0
    ordered_occ = occ_ints
    if not rows:
        ordered_occ = order_columns(order_rows(occ_ints, n, position & 1), n, position & 1)
    core = (position & 1).astype(jnp.int32).reshape(1)
    own_denom = denom[:, 0, :]
    resps = [rhs[:, state, :] / own_denom for state in range(states)]
    for step in range(ITERS):
        got = [gather_rows(resp.astype(jnp.bfloat16), n) for resp in resps]
        keep, send = exchange_part(core, ordered_occ, [g[0] for g in got], [g[1] for g in got], vir_ints, rows)
        for state in range(states):
            exchange = scatter_sum(keep[state], send[state], n)
            resps[state] = 0.4 * resps[state] + 0.6 * (rhs[:, state, :] - exchange) / own_denom
    response = jnp.stack(resps, axis=1)
    return response


def solution(mesh):
    in_specs = (
        P(("grp", "aux"), None, None),
        P("grp"),
        P("grp"),
        P(("grp", "aux"), None, None),
        P(("grp", "aux"), None, None),
    )
    out_specs = P(("grp", "aux"), None, None)
    return jax.shard_map(shards, mesh=mesh, in_specs=in_specs, out_specs=out_specs, check_vma=False)
```
